256 devices in a mesh: seq: 64 (over x, z, core), ch: 4 (over y).
Axes of the slice: x: 4, y: 4, z: 8, core: 2. Of those that a mesh axis runs over, the one named last changes fastest.
Arguments:
- inputs: bfloat16 [8192, 4096], P('seq'), may hold values from -6 to 6
- norm_gain: float32 [4096], replicated, may hold values from 0.1 to 1.9
- in_weight: bfloat16 [4096, 3, 1024], P('seq', None, 'ch'), may hold values from -0.09375 to 0.09375
- short_filter: float32 [3, 3, 1024], P(None, None, 'ch'), may hold values from -4 to 4
- long_filter: float32 [8192, 1024], P('seq', 'ch'), may hold values from -2.2 to 2.2
- conv_bias: float32 [1024], P('ch'), may hold values from -4 to 4
- out_weight: bfloat16 [1024, 4096], P('ch', 'seq'), may hold values from -0.1875 to 0.1875
- out_grad: bfloat16 [8192, 4096], P('seq'), may hold values from -6 to 6
Outputs:
- block_out: bfloat16 [8192, 4096], P('seq', 'ch')
- in_grad: bfloat16 [8192, 4096], P('seq')
- filter_grad: float32 [8192, 1024], P('seq', 'ch')
The draws below stay inside these ranges and needn't reach their ends.
All inputs are finite; a program needn't handle non-finite values.
Results may differ from the reference program's by a relative error of at most 0.013.
Values may be sent and summed in bfloat16 or wider, within the bound.
No kernel may reach another device: no remote copies, remote signals or barrier semaphores. Data moves between devices by JAX's collectives and lax.ppermute only.
A program may use at most 64 MiB of HBM per device.

```python
import math
import jax
import jax.numpy as jnp
from jax import lax

D = 4096
C = 1024
KS = 3
SEQ_LEN = 8192


def draw_long_filter(key, part):
    rate_key, noise_key = jax.random.split(key)
    lowest = math.log(8.0)
    highest_span = math.log(4.0 * SEQ_LEN)
    spans = jnp.exp(jax.random.uniform(rate_key, (C,), jnp.float32, lowest, highest_span))
    places = jnp.arange(SEQ_LEN, dtype=jnp.float32)[:, None]
    noise = jnp.clip(jax.random.normal(noise_key, (SEQ_LEN, C), jnp.float32), -6.0, 6.0)
    return noise * jnp.exp(-places / spans[None, :]) / jnp.sqrt(spans)[None, :]


def shard_levels(stream_key, dims, pieces, smallest, top_value):
    loudness = 1.0
    for position, parts in pieces:
        steps = jax.random.uniform(jax.random.fold_in(jax.random.fold_in(stream_key, 6), position), (parts,), jnp.float32, smallest / len(pieces), top_value / len(pieces))
        loudness = loudness * jnp.repeat(jnp.exp(steps), dims[position] // parts).reshape((-1,) + (1,) * (len(dims) - 1 - position))
    return loudness


def centred(stream_key, dims, spread, reach, pieces=(), kind=jnp.bfloat16):
    level = shard_levels(stream_key, dims, pieces, -0.22, 0.18) if pieces else 1.0
    values = jax.random.normal(stream_key, dims, jnp.float32) * spread * level
    return jnp.minimum(jnp.maximum(values, -reach), reach).astype(kind)


def setup_inputs(seed: int = 0) -> dict:
    streams_of = jax.random.split(jax.random.key(seed), 9)
    inputs = centred(streams_of[0], (SEQ_LEN, D), 1.0, 6.0, ((0, 64),))
    norm_gain = jnp.clip(1.0 + 0.18 * jax.random.normal(streams_of[1], (D,), jnp.float32), 0.1, 1.9)
    in_weight = centred(streams_of[2], (D, 3, C), D ** -0.5, 0.09375, ((0, 64), (2, 4)))
    short_filter = centred(streams_of[3], (3, KS, C), 0.6, 4.0, ((2, 4),), jnp.float32)
    long_filter = draw_long_filter(jax.random.fold_in(streams_of[8], 71), 0)
    conv_bias = centred(streams_of[5], (C,), 1.0, 4.0, ((0, 4),), jnp.float32)
    out_weight = centred(streams_of[6], (C, D), C ** -0.5, 0.1875, ((0, 4), (1, 64)))
    out_grad = centred(streams_of[7], (SEQ_LEN, D), 1.0, 6.0, ((0, 64),))
    return dict(inputs=inputs, norm_gain=norm_gain, in_weight=in_weight, short_filter=short_filter, long_filter=long_filter, conv_bias=conv_bias, out_weight=out_weight, out_grad=out_grad)


epsilon = 1e-05

def short_forward(projected, short_filter):
    running = jnp.zeros(projected.shape, jnp.float32)
    for offset in range(KS):
        moved = jnp.pad(projected, ((offset, 0), (0, 0), (0, 0)))[:projected.shape[0]]
        running = running + short_filter[:, offset, :][None] * moved
    return running

def short_backward(mixed_grad, short_filter):
    running = jnp.zeros(mixed_grad.shape, jnp.float32)
    for offset in range(KS):
        moved = jnp.pad(mixed_grad, ((0, offset), (0, 0), (0, 0)))[offset:]
        running = running + short_filter[:, offset, :][None] * moved
    return running

def spectral_ops(product, long_filter, carried):
    padded_len = 2 * SEQ_LEN
    spec_signal = jnp.fft.rfft(product, n=padded_len, axis=0)
    spec_filter = jnp.fft.rfft(long_filter, n=padded_len, axis=0)
    spec_grad = jnp.fft.rfft(carried, n=padded_len, axis=0)
    conv_out = jnp.fft.irfft(spec_signal * spec_filter, n=padded_len, axis=0)[:SEQ_LEN]
    back_conv = jnp.fft.irfft(spec_grad * jnp.conj(spec_filter), n=padded_len, axis=0)[:SEQ_LEN]
    filter_sum = jnp.fft.irfft(spec_grad * jnp.conj(spec_signal), n=padded_len, axis=0)[:SEQ_LEN]
    return (conv_out.astype(jnp.float32), back_conv.astype(jnp.float32), filter_sum.astype(jnp.float32))

def reference(inputs, norm_gain, in_weight, short_filter, long_filter, conv_bias, out_weight, out_grad):
    wide_inputs = inputs.astype(jnp.float32)
    inv_rms = lax.rsqrt(lax.optimization_barrier(jnp.mean(wide_inputs * wide_inputs, axis=1, keepdims=True)) + epsilon)
    normed = (wide_inputs * inv_rms * norm_gain).astype(jnp.bfloat16)
    in_flat = in_weight.reshape(D, 3 * C)
    projected = jnp.dot(normed, in_flat, preferred_element_type=jnp.float32).astype(jnp.bfloat16)
    projected = projected.reshape(SEQ_LEN, 3, C).astype(jnp.float32)
    mixed = short_forward(projected, short_filter)
    query_br = mixed[:, 0]
    key_br = mixed[:, 1]
    value_br = mixed[:, 2]
    product = key_br * value_br
    gate_grad = jnp.dot(out_grad, out_weight.T, preferred_element_type=jnp.float32)
    carried = gate_grad * query_br
    conv_out, back_conv, filter_sum = spectral_ops(product, long_filter, carried)
    biased = conv_out + conv_bias * product
    gated = (query_br * biased).astype(jnp.bfloat16)
    block_out = (wide_inputs + jnp.dot(gated, out_weight, preferred_element_type=jnp.float32)).astype(jnp.bfloat16)
    filter_grad = filter_sum * SEQ_LEN ** (-0.5)
    source_grad = back_conv + conv_bias * carried
    mixed_grad = jnp.stack([gate_grad * biased, source_grad * value_br, source_grad * key_br], axis=1)
    proj_grad = short_backward(mixed_grad, short_filter).astype(jnp.bfloat16).reshape(SEQ_LEN, 3 * C)
    norm_grad = jnp.dot(proj_grad, in_flat.T, preferred_element_type=jnp.float32)
    weighted = norm_grad * norm_gain
    inner_term = lax.optimization_barrier(jnp.mean(weighted * wide_inputs, axis=1, keepdims=True))
    in_grad = (out_grad.astype(jnp.float32) + weighted * inv_rms - wide_inputs * inv_rms ** 3 * inner_term).astype(jnp.bfloat16)
    return (block_out, in_grad, filter_grad)
```

```python
import math

import jax
import jax.numpy as jnp
from jax import lax
from jax.sharding import PartitionSpec as P

epsilon = 1e-05
highest = lax.Precision.HIGHEST


def passed_along(block, axis, distance):
    devices = range(lax.axis_size(axis))
    route = [(i - distance, i) for i in devices if i - distance in devices]
    return lax.ppermute(block, axis, route)


def to_columns(signals):
    return lax.all_to_all(signals, "seq", split_axis=1, concat_axis=2, tiled=True)


def to_rows(signals):
    return lax.all_to_all(signals, "seq", split_axis=2, concat_axis=1, tiled=True)


def turn_table(rows, cols, period, sign):
    turns = jnp.arange(rows, dtype=jnp.int32)[:, None] * jnp.arange(cols, dtype=jnp.int32)[None, :]
    phases = sign * 2.0 * math.pi / period * (turns % period).astype(jnp.float32)
    return (jnp.cos(phases), jnp.sin(phases))


def fft_sizes(seq_total):
    total = 2 * seq_total
    inner = 1
    while inner * inner < total:
        inner *= 2
    return total // inner, inner


def forward_dft(signals):
    count, chans, seq_total = signals.shape
    outer, inner = fft_sizes(seq_total)
    grid = signals.reshape(count, chans, outer // 2, inner)
    cos_out, sin_out = turn_table(outer, outer // 2, outer, 1.0)
    first_real = jnp.einsum("kn,ucnm->uckm", cos_out, grid, precision=highest)
    first_imag = -jnp.einsum("kn,ucnm->uckm", sin_out, grid, precision=highest)
    cos_tw, sin_tw = turn_table(outer, inner, outer * inner, 1.0)
    turned_real = first_real * cos_tw + first_imag * sin_tw
    turned_imag = first_imag * cos_tw - first_real * sin_tw
    cos_in, sin_in = turn_table(inner, inner, inner, 1.0)
    spec_real = jnp.einsum("uckm,mj->uckj", turned_real, cos_in, precision=highest) + jnp.einsum(
        "uckm,mj->uckj", turned_imag, sin_in, precision=highest
    )
    spec_imag = jnp.einsum("uckm,mj->uckj", turned_imag, cos_in, precision=highest) - jnp.einsum(
        "uckm,mj->uckj", turned_real, sin_in, precision=highest
    )
    return spec_real, spec_imag


def inverse_dft(spec_real, spec_imag):
    count, chans, outer, inner = spec_real.shape
    cos_in, sin_in = turn_table(inner, inner, inner, 1.0)
    back_real = jnp.einsum("uckj,jm->uckm", spec_real, cos_in, precision=highest) - jnp.einsum(
        "uckj,jm->uckm", spec_imag, sin_in, precision=highest
    )
    back_imag = jnp.einsum("uckj,jm->uckm", spec_imag, cos_in, precision=highest) + jnp.einsum(
        "uckj,jm->uckm", spec_real, sin_in, precision=highest
    )
    cos_tw, sin_tw = turn_table(outer, inner, outer * inner, 1.0)
    turned_real = back_real * cos_tw - back_imag * sin_tw
    turned_imag = back_imag * cos_tw + back_real * sin_tw
    cos_out, sin_out = turn_table(outer, outer // 2, outer, 1.0)
    grid = jnp.einsum("kn,uckm->ucnm", cos_out, turned_real, precision=highest) - jnp.einsum(
        "kn,uckm->ucnm", sin_out, turned_imag, precision=highest
    )
    return grid.reshape(count, chans, outer * inner // 2) / float(outer * inner)


def per_device(
    inputs, norm_gain, in_weight, short_filter, long_filter, conv_bias, out_weight, out_grad
):
    local_rows = inputs.shape[0]
    model_width = inputs.shape[1]
    slab_width = long_filter.shape[1]
    taps = short_filter.shape[1]
    wide_inputs = inputs.astype(jnp.float32)
    inv_rms = lax.rsqrt(jnp.mean(wide_inputs * wide_inputs, axis=1, keepdims=True) + epsilon)
    normed = (wide_inputs * inv_rms * norm_gain).astype(jnp.bfloat16)
    in_panel, out_panel = (
        lax.all_gather(in_weight, "seq", axis=0, tiled=True),
        lax.all_gather(out_weight, "seq", axis=1, tiled=True),
    )
    in_flat = in_panel.reshape(model_width, 3 * slab_width)
    projected = jnp.dot(normed, in_flat, preferred_element_type=jnp.float32)
    projected = projected.astype(jnp.bfloat16).reshape(local_rows, 3, slab_width)
    upper_rim = passed_along(projected[local_rows - (taps - 1) :], "seq", 1)
    extended = jnp.concatenate([upper_rim, projected], 0).astype(jnp.float32)
    mixed = jnp.zeros((local_rows, 3, slab_width), jnp.float32)
    for offset in range(taps):
        begin = taps - 1 - offset
        mixed = mixed + short_filter[:, offset, :][None] * extended[begin : begin + local_rows]
    query_br = mixed[:, 0]
    key_br = mixed[:, 1]
    value_br = mixed[:, 2]
    product = key_br * value_br
    gate_grad = jnp.dot(out_grad, out_panel.T, preferred_element_type=jnp.float32)
    carried = gate_grad * query_br
    columns = to_columns(jnp.stack([product, long_filter, carried]).transpose(0, 2, 1))
    all_real, all_imag = forward_dft(columns)
    sig_real, filt_real, grad_real = (all_real[0], all_real[1], all_real[2])
    sig_imag, filt_imag, grad_imag = (all_imag[0], all_imag[1], all_imag[2])
    conv_real = sig_real * filt_real - sig_imag * filt_imag
    conv_imag = sig_real * filt_imag + sig_imag * filt_real
    back_real = grad_real * filt_real + grad_imag * filt_imag
    back_imag = grad_imag * filt_real - grad_real * filt_imag
    pair_real = grad_real * sig_real + grad_imag * sig_imag
    pair_imag = grad_imag * sig_real - grad_real * sig_imag
    outs = inverse_dft(
        jnp.stack([conv_real, back_real, pair_real]), jnp.stack([conv_imag, back_imag, pair_imag])
    )
    returned = to_rows(outs).transpose(0, 2, 1)
    conv_out = returned[0]
    back_conv = returned[1]
    filter_grad = returned[2] * float(local_rows * lax.axis_size("seq")) ** (-0.5)
    biased = conv_out + conv_bias * product
    gated = (query_br * biased).astype(jnp.bfloat16)
    partial_out = jnp.dot(gated, out_panel, preferred_element_type=jnp.float32)
    summed = lax.psum_scatter(
        partial_out.astype(jnp.bfloat16), "ch", scatter_dimension=1, tiled=True
    ).astype(jnp.float32)
    share = summed.shape[1]
    residual = lax.dynamic_slice_in_dim(wide_inputs, lax.axis_index("ch") * share, share, 1)
    block_out = (residual + summed).astype(jnp.bfloat16)
    source_grad = back_conv + conv_bias * carried
    mixed_grad = jnp.stack([gate_grad * biased, source_grad * value_br, source_grad * key_br], 1)
    lower_rim = passed_along(mixed_grad[: taps - 1], "seq", -1)
    extended_back = jnp.concatenate([mixed_grad, lower_rim], 0)
    proj_grad = jnp.zeros((local_rows, 3, slab_width), jnp.float32)
    for offset in range(taps):
        proj_grad = (
            proj_grad
            + short_filter[:, offset, :][None] * extended_back[offset : offset + local_rows]
        )
    proj_grad = proj_grad.astype(jnp.bfloat16).reshape(local_rows, 3 * slab_width)
    partial_grad = jnp.dot(proj_grad, in_flat.T, preferred_element_type=jnp.float32)
    norm_grad = lax.psum(partial_grad, "ch")
    weighted = norm_grad * norm_gain
    inner_term = jnp.mean(weighted * wide_inputs, axis=1, keepdims=True)
    in_grad = (
        out_grad.astype(jnp.float32) + weighted * inv_rms - wide_inputs * inv_rms**3 * inner_term
    ).astype(jnp.bfloat16)
    return (block_out, in_grad, filter_grad)


def solution(mesh):
    return jax.shard_map(
        per_device,
        mesh=mesh,
        in_specs=(
            P("seq", None),
            P(),
            P("seq", None, "ch"),
            P(None, None, "ch"),
            P("seq", "ch"),
            P("ch"),
            P("ch", "seq"),
            P("seq", None),
        ),
        out_specs=(P("seq", "ch"), P("seq", None), P("seq", "ch")),
        check_vma=False,
    )
```

```python
import math

import jax
import jax.numpy as jnp
from jax import lax
from jax.sharding import PartitionSpec as P

epsilon = 1e-05
highest = lax.Precision.HIGHEST


def passed_along(block, axis, distance):
    devices = range(lax.axis_size(axis))
    route = [(i - distance, i) for i in devices if i - distance in devices]
    return lax.ppermute(block, axis, route)


def to_columns(signals):
    return lax.all_to_all(signals, "seq", split_axis=1, concat_axis=2, tiled=True)


def to_rows(signals):
    count, chans, seq_total = signals.shape
    devices = lax.axis_size("seq")
    local_rows = seq_total // devices
    pieces = signals.reshape(count, chans, devices, local_rows).transpose(2, 0, 1, 3)
    arrived = lax.all_to_all(pieces, "seq", split_axis=0, concat_axis=0, tiled=True)
    return arrived.transpose(1, 3, 0, 2).reshape(count, local_rows, devices * chans)


def turn_table(rows, cols, period, sign):
    turns = jnp.arange(rows, dtype=jnp.int32)[:, None] * jnp.arange(cols, dtype=jnp.int32)[None, :]
    phases = sign * 2.0 * math.pi / period * (turns % period).astype(jnp.float32)
    return (jnp.cos(phases), jnp.sin(phases))


def fft_sizes(seq_total):
    total = 2 * seq_total
    inner = 1
    while inner * inner < total:
        inner *= 2
    return total // inner, inner


def forward_dft(signals):
    count, chans, seq_total = signals.shape
    outer, inner = fft_sizes(seq_total)
    grid = signals.reshape(count, chans, outer // 2, inner)
    cos_out, sin_out = turn_table(outer, outer // 2, outer, 1.0)
    first_real = jnp.einsum("kn,ucnm->uckm", cos_out, grid, precision=highest)
    first_imag = -jnp.einsum("kn,ucnm->uckm", sin_out, grid, precision=highest)
    cos_tw, sin_tw = turn_table(outer, inner, outer * inner, 1.0)
    turned_real = first_real * cos_tw + first_imag * sin_tw
    turned_imag = first_imag * cos_tw - first_real * sin_tw
    cos_in, sin_in = turn_table(inner, inner, inner, 1.0)
    spec_real = jnp.einsum("uckm,mj->uckj", turned_real, cos_in, precision=highest) + jnp.einsum(
        "uckm,mj->uckj", turned_imag, sin_in, precision=highest
    )
    spec_imag = jnp.einsum("uckm,mj->uckj", turned_imag, cos_in, precision=highest) - jnp.einsum(
        "uckm,mj->uckj", turned_real, sin_in, precision=highest
    )
    return spec_real, spec_imag


def inverse_dft(spec_real, spec_imag):
    count, chans, outer, inner = spec_real.shape
    cos_in, sin_in = turn_table(inner, inner, inner, 1.0)
    back_real = jnp.einsum("uckj,jm->uckm", spec_real, cos_in, precision=highest) - jnp.einsum(
        "uckj,jm->uckm", spec_imag, sin_in, precision=highest
    )
    back_imag = jnp.einsum("uckj,jm->uckm", spec_imag, cos_in, precision=highest) + jnp.einsum(
        "uckj,jm->uckm", spec_real, sin_in, precision=highest
    )
    cos_tw, sin_tw = turn_table(outer, inner, outer * inner, 1.0)
    turned_real = back_real * cos_tw - back_imag * sin_tw
    turned_imag = back_imag * cos_tw + back_real * sin_tw
    cos_out, sin_out = turn_table(outer, outer // 2, outer, 1.0)
    grid = jnp.einsum("kn,uckm->ucnm", cos_out, turned_real, precision=highest) - jnp.einsum(
        "kn,uckm->ucnm", sin_out, turned_imag, precision=highest
    )
    return grid.reshape(count, chans, outer * inner // 2) / float(outer * inner)


def per_device(
    inputs, norm_gain, in_weight, short_filter, long_filter, conv_bias, out_weight, out_grad
):
    local_rows = inputs.shape[0]
    model_width = inputs.shape[1]
    slab_width = long_filter.shape[1]
    taps = short_filter.shape[1]
    wide_inputs = inputs.astype(jnp.float32)
    inv_rms = lax.rsqrt(jnp.mean(wide_inputs * wide_inputs, axis=1, keepdims=True) + epsilon)
    normed = (wide_inputs * inv_rms * norm_gain).astype(jnp.bfloat16)
    in_panel, out_panel = (
        lax.all_gather(in_weight, "seq", axis=0, tiled=True),
        lax.all_gather(out_weight, "seq", axis=1, tiled=True),
    )
    in_flat = in_panel.reshape(model_width, 3 * slab_width)
    projected = jnp.dot(normed, in_flat, preferred_element_type=jnp.float32)
    projected = projected.astype(jnp.bfloat16).reshape(local_rows, 3, slab_width)
    upper_rim = passed_along(projected[local_rows - (taps - 1) :], "seq", 1)
    extended = jnp.concatenate([upper_rim, projected], 0).astype(jnp.float32)
    mixed = jnp.zeros((local_rows, 3, slab_width), jnp.float32)
    for offset in range(taps):
        begin = taps - 1 - offset
        mixed = mixed + short_filter[:, offset, :][None] * extended[begin : begin + local_rows]
    query_br = mixed[:, 0]
    key_br = mixed[:, 1]
    value_br = mixed[:, 2]
    product = key_br * value_br
    gate_grad = jnp.dot(out_grad, out_panel.T, preferred_element_type=jnp.float32)
    carried = gate_grad * query_br
    columns = to_columns(jnp.stack([product, long_filter, carried]).transpose(0, 2, 1))
    all_real, all_imag = forward_dft(columns)
    sig_real, filt_real, grad_real = (all_real[0], all_real[1], all_real[2])
    sig_imag, filt_imag, grad_imag = (all_imag[0], all_imag[1], all_imag[2])
    conv_real = sig_real * filt_real - sig_imag * filt_imag
    conv_imag = sig_real * filt_imag + sig_imag * filt_real
    back_real = grad_real * filt_real + grad_imag * filt_imag
    back_imag = grad_imag * filt_real - grad_real * filt_imag
    pair_real = grad_real * sig_real + grad_imag * sig_imag
    pair_imag = grad_imag * sig_real - grad_real * sig_imag
    outs = inverse_dft(
        jnp.stack([conv_real, back_real, pair_real]), jnp.stack([conv_imag, back_imag, pair_imag])
    )
    returned = to_rows(outs)
    conv_out = returned[0]
    back_conv = returned[1]
    filter_grad = returned[2] * float(local_rows * lax.axis_size("seq")) ** (-0.5)
    biased = conv_out + conv_bias * product
    gated = (query_br * biased).astype(jnp.bfloat16)
    partial_out = jnp.dot(gated, out_panel, preferred_element_type=jnp.float32)
    summed = lax.psum_scatter(
        partial_out.astype(jnp.bfloat16), "ch", scatter_dimension=1, tiled=True
    ).astype(jnp.float32)
    share = summed.shape[1]
    residual = lax.dynamic_slice_in_dim(wide_inputs, lax.axis_index("ch") * share, share, 1)
    block_out = (residual + summed).astype(jnp.bfloat16)
    source_grad = back_conv + conv_bias * carried
    mixed_grad = jnp.stack([gate_grad * biased, source_grad * value_br, source_grad * key_br], 1)
    lower_rim = passed_along(mixed_grad[: taps - 1], "seq", -1)
    extended_back = jnp.concatenate([mixed_grad, lower_rim], 0)
    proj_grad = jnp.zeros((local_rows, 3, slab_width), jnp.float32)
    for offset in range(taps):
        proj_grad = (
            proj_grad
            + short_filter[:, offset, :][None] * extended_back[offset : offset + local_rows]
        )
    proj_grad = proj_grad.astype(jnp.bfloat16).reshape(local_rows, 3 * slab_width)
    partial_grad = jnp.dot(proj_grad, in_flat.T, preferred_element_type=jnp.float32)
    norm_grad = lax.psum_scatter(
        partial_grad.astype(jnp.bfloat16), "ch", scatter_dimension=1, tiled=True
    ).astype(jnp.float32)
    feature_share = norm_grad.shape[1]
    feature_begin = lax.axis_index("ch") * feature_share
    gain_share = lax.dynamic_slice_in_dim(norm_gain, feature_begin, feature_share, 0)
    inputs_share = lax.dynamic_slice_in_dim(wide_inputs, feature_begin, feature_share, 1)
    grad_share = lax.dynamic_slice_in_dim(out_grad, feature_begin, feature_share, 1)
    weighted = norm_grad * gain_share
    inner_term = lax.psum(jnp.sum(weighted * inputs_share, axis=1, keepdims=True), "ch") / model_width
    in_grad_share = (
        grad_share.astype(jnp.float32) + weighted * inv_rms - inputs_share * inv_rms**3 * inner_term
    ).astype(jnp.bfloat16)
    in_grad = lax.all_gather(in_grad_share, "ch", axis=1, tiled=True)
    return (block_out, in_grad, filter_grad)


def solution(mesh):
    return jax.shard_map(
        per_device,
        mesh=mesh,
        in_specs=(
            P("seq", None),
            P(),
            P("seq", None, "ch"),
            P(None, None, "ch"),
            P("seq", "ch"),
            P("ch"),
            P("ch", "seq"),
            P("seq", None),
        ),
        out_specs=(P("seq", "ch"), P("seq", None), P("seq", "ch")),
        check_vma=False,
    )
```

```python
import math

import jax
import jax.numpy as jnp
from jax import lax
from jax.sharding import PartitionSpec as P

epsilon = 1e-05
highest = lax.Precision.HIGHEST
SEQ = ("chips", "core")
CORES = 2


def passed_along(block, axis, distance):
    devices = range(lax.axis_size(axis))
    route = [(i - distance, i) for i in devices if i - distance in devices]
    return lax.ppermute(block, axis, route)


def to_columns(signals):
    return lax.all_to_all(signals, SEQ, split_axis=1, concat_axis=2, tiled=True)


def to_rows(signals):
    count, chans, seq_total = signals.shape
    devices = lax.axis_size(SEQ)
    local_rows = seq_total // devices
    pieces = signals.reshape(count, chans, devices, local_rows).transpose(2, 0, 1, 3)
    arrived = lax.all_to_all(pieces, SEQ, split_axis=0, concat_axis=0, tiled=True)
    return arrived.transpose(1, 3, 0, 2).reshape(count, local_rows, devices * chans)


def turn_table(rows, cols, period, sign):
    turns = jnp.arange(rows, dtype=jnp.int32)[:, None] * jnp.arange(cols, dtype=jnp.int32)[None, :]
    phases = sign * 2.0 * math.pi / period * (turns % period).astype(jnp.float32)
    return (jnp.cos(phases), jnp.sin(phases))


def fft_sizes(seq_total):
    total = 2 * seq_total
    inner = 1
    while inner * inner < total:
        inner *= 2
    return total // inner, inner


def forward_dft(signals):
    count, chans, seq_total = signals.shape
    outer, inner = fft_sizes(seq_total)
    grid = signals.reshape(count, chans, outer // 2, inner)
    cos_out, sin_out = turn_table(outer, outer // 2, outer, 1.0)
    first_real = jnp.einsum("kn,ucnm->uckm", cos_out, grid, precision=highest)
    first_imag = -jnp.einsum("kn,ucnm->uckm", sin_out, grid, precision=highest)
    cos_tw, sin_tw = turn_table(outer, inner, outer * inner, 1.0)
    turned_real = first_real * cos_tw + first_imag * sin_tw
    turned_imag = first_imag * cos_tw - first_real * sin_tw
    cos_in, sin_in = turn_table(inner, inner, inner, 1.0)
    spec_real = jnp.einsum("uckm,mj->uckj", turned_real, cos_in, precision=highest) + jnp.einsum(
        "uckm,mj->uckj", turned_imag, sin_in, precision=highest
    )
    spec_imag = jnp.einsum("uckm,mj->uckj", turned_imag, cos_in, precision=highest) - jnp.einsum(
        "uckm,mj->uckj", turned_real, sin_in, precision=highest
    )
    return spec_real, spec_imag


def inverse_dft(spec_real, spec_imag):
    count, chans, outer, inner = spec_real.shape
    cos_in, sin_in = turn_table(inner, inner, inner, 1.0)
    back_real = jnp.einsum("uckj,jm->uckm", spec_real, cos_in, precision=highest) - jnp.einsum(
        "uckj,jm->uckm", spec_imag, sin_in, precision=highest
    )
    back_imag = jnp.einsum("uckj,jm->uckm", spec_imag, cos_in, precision=highest) + jnp.einsum(
        "uckj,jm->uckm", spec_real, sin_in, precision=highest
    )
    cos_tw, sin_tw = turn_table(outer, inner, outer * inner, 1.0)
    turned_real = back_real * cos_tw - back_imag * sin_tw
    turned_imag = back_imag * cos_tw + back_real * sin_tw
    cos_out, sin_out = turn_table(outer, outer // 2, outer, 1.0)
    grid = jnp.einsum("kn,uckm->ucnm", cos_out, turned_real, precision=highest) - jnp.einsum(
        "kn,uckm->ucnm", sin_out, turned_imag, precision=highest
    )
    return grid.reshape(count, chans, outer * inner // 2) / float(outer * inner)


def per_device(
    inputs, norm_gain, in_weight, short_filter, long_filter, conv_bias, out_weight, out_grad
):
    local_rows = inputs.shape[0]
    model_width = inputs.shape[1]
    slab_width = long_filter.shape[1]
    taps = short_filter.shape[1]
    wide_inputs = inputs.astype(jnp.float32)
    inv_rms = lax.rsqrt(jnp.mean(wide_inputs * wide_inputs, axis=1, keepdims=True) + epsilon)
    normed = (wide_inputs * inv_rms * norm_gain).astype(jnp.bfloat16)
    in_half = lax.all_gather(in_weight, "chips", axis=0)
    in_panel = lax.all_gather(in_half, "core", axis=1).reshape(model_width, 3, slab_width)
    out_half = lax.all_gather(out_weight, "chips", axis=1)
    out_panel = lax.all_gather(out_half, "core", axis=2).reshape(slab_width, model_width)
    in_flat = in_panel.reshape(model_width, 3 * slab_width)
    projected = jnp.dot(normed, in_flat, preferred_element_type=jnp.float32)
    projected = projected.astype(jnp.bfloat16).reshape(local_rows, 3, slab_width)
    upper_rim = passed_along(projected[local_rows - (taps - 1) :], SEQ, 1)
    extended = jnp.concatenate([upper_rim, projected], 0).astype(jnp.float32)
    mixed = jnp.zeros((local_rows, 3, slab_width), jnp.float32)
    for offset in range(taps):
        begin = taps - 1 - offset
        mixed = mixed + short_filter[:, offset, :][None] * extended[begin : begin + local_rows]
    query_br = mixed[:, 0]
    key_br = mixed[:, 1]
    value_br = mixed[:, 2]
    product = key_br * value_br
    gate_grad = jnp.dot(out_grad, out_panel.T, preferred_element_type=jnp.float32)
    carried = gate_grad * query_br
    columns = to_columns(jnp.stack([product, long_filter, carried]).transpose(0, 2, 1))
    all_real, all_imag = forward_dft(columns)
    sig_real, filt_real, grad_real = (all_real[0], all_real[1], all_real[2])
    sig_imag, filt_imag, grad_imag = (all_imag[0], all_imag[1], all_imag[2])
    conv_real = sig_real * filt_real - sig_imag * filt_imag
    conv_imag = sig_real * filt_imag + sig_imag * filt_real
    back_real = grad_real * filt_real + grad_imag * filt_imag
    back_imag = grad_imag * filt_real - grad_real * filt_imag
    pair_real = grad_real * sig_real + grad_imag * sig_imag
    pair_imag = grad_imag * sig_real - grad_real * sig_imag
    outs = inverse_dft(
        jnp.stack([conv_real, back_real, pair_real]), jnp.stack([conv_imag, back_imag, pair_imag])
    )
    returned = to_rows(outs)
    conv_out = returned[0]
    back_conv = returned[1]
    filter_grad = returned[2] * float(local_rows * lax.axis_size(SEQ)) ** (-0.5)
    biased = conv_out + conv_bias * product
    gated = (query_br * biased).astype(jnp.bfloat16)
    partial_out = jnp.dot(gated, out_panel, preferred_element_type=jnp.float32)
    summed = lax.psum_scatter(
        partial_out.astype(jnp.bfloat16), "ch", scatter_dimension=1, tiled=True
    ).astype(jnp.float32)
    share = summed.shape[1]
    residual = lax.dynamic_slice_in_dim(wide_inputs, lax.axis_index("ch") * share, share, 1)
    block_out = (residual + summed).astype(jnp.bfloat16)
    source_grad = back_conv + conv_bias * carried
    mixed_grad = jnp.stack([gate_grad * biased, source_grad * value_br, source_grad * key_br], 1)
    lower_rim = passed_along(mixed_grad[: taps - 1], SEQ, -1)
    extended_back = jnp.concatenate([mixed_grad, lower_rim], 0)
    proj_grad = jnp.zeros((local_rows, 3, slab_width), jnp.float32)
    for offset in range(taps):
        proj_grad = (
            proj_grad
            + short_filter[:, offset, :][None] * extended_back[offset : offset + local_rows]
        )
    proj_grad = proj_grad.astype(jnp.bfloat16).reshape(local_rows, 3 * slab_width)
    partial_grad = jnp.dot(proj_grad, in_flat.T, preferred_element_type=jnp.float32)
    norm_grad = lax.psum_scatter(
        partial_grad.astype(jnp.bfloat16), "ch", scatter_dimension=1, tiled=True
    ).astype(jnp.float32)
    feature_share = norm_grad.shape[1]
    feature_begin = lax.axis_index("ch") * feature_share
    gain_share = lax.dynamic_slice_in_dim(norm_gain, feature_begin, feature_share, 0)
    inputs_share = lax.dynamic_slice_in_dim(wide_inputs, feature_begin, feature_share, 1)
    grad_share = lax.dynamic_slice_in_dim(out_grad, feature_begin, feature_share, 1)
    weighted = norm_grad * gain_share
    inner_term = lax.psum(jnp.sum(weighted * inputs_share, axis=1, keepdims=True), "ch") / model_width
    in_grad_share = (
        grad_share.astype(jnp.float32) + weighted * inv_rms - inputs_share * inv_rms**3 * inner_term
    ).astype(jnp.bfloat16)
    in_grad = lax.all_gather(in_grad_share, "ch", axis=1, tiled=True)
    return (block_out, in_grad, filter_grad)


def solution(mesh):
    seq_size, ch_size = mesh.devices.shape
    split_mesh = jax.sharding.Mesh(
        mesh.devices.reshape(seq_size // CORES, CORES, ch_size), ("chips", "core", "ch")
    )
    return jax.shard_map(
        per_device,
        mesh=split_mesh,
        in_specs=(
            P(SEQ, None),
            P(),
            P(SEQ, None, "ch"),
            P(None, None, "ch"),
            P(SEQ, "ch"),
            P("ch"),
            P("ch", SEQ),
            P(SEQ, None),
        ),
        out_specs=(P(SEQ, "ch"), P(SEQ, None), P(SEQ, "ch")),
        check_vma=False,
    )
```

```python
import math

import jax
import jax.numpy as jnp
from jax import lax
from jax.sharding import PartitionSpec as P

epsilon = 1e-05
highest = lax.Precision.HIGHEST


def passed_along(block, axis, distance):
    devices = range(lax.axis_size(axis))
    route = [(i - distance, i) for i in devices if i - distance in devices]
    return lax.ppermute(block, axis, route)


def doubled_gather(block, axis):
    devices = lax.axis_size(axis)
    place = lax.axis_index(axis)
    bits = devices.bit_length() - 1
    assert 1 << bits == devices
    gathered = block
    for bit in reversed(range(bits)):
        route = [(i, i ^ (1 << bit)) for i in range(devices)]
        arrived = lax.ppermute(gathered, axis, route)
        lower = ((place >> bit) & 1) == 0
        gathered = jnp.where(lower, jnp.stack([gathered, arrived]), jnp.stack([arrived, gathered]))
    gathered = gathered.transpose(tuple(reversed(range(bits))) + tuple(range(bits, gathered.ndim)))
    return gathered.reshape((devices * block.shape[0],) + block.shape[1:])


def to_columns(signals):
    return lax.all_to_all(signals, "seq", split_axis=1, concat_axis=2, tiled=True)


def to_rows(signals):
    count, chans, seq_total = signals.shape
    devices = lax.axis_size("seq")
    local_rows = seq_total // devices
    pieces = signals.reshape(count, chans, devices, local_rows).transpose(2, 0, 1, 3)
    arrived = lax.all_to_all(pieces, "seq", split_axis=0, concat_axis=0, tiled=True)
    return arrived.transpose(1, 3, 0, 2).reshape(count, local_rows, devices * chans)


def turn_table(rows, cols, period, sign):
    turns = jnp.arange(rows, dtype=jnp.int32)[:, None] * jnp.arange(cols, dtype=jnp.int32)[None, :]
    phases = sign * 2.0 * math.pi / period * (turns % period).astype(jnp.float32)
    return (jnp.cos(phases), jnp.sin(phases))


def fft_sizes(seq_total):
    total = 2 * seq_total
    inner = 1
    while inner * inner < total:
        inner *= 2
    return total // inner, inner


def forward_dft(signals):
    count, chans, seq_total = signals.shape
    outer, inner = fft_sizes(seq_total)
    grid = signals.reshape(count, chans, outer // 2, inner)
    cos_out, sin_out = turn_table(outer, outer // 2, outer, 1.0)
    first_real = jnp.einsum("kn,ucnm->uckm", cos_out, grid, precision=highest)
    first_imag = -jnp.einsum("kn,ucnm->uckm", sin_out, grid, precision=highest)
    cos_tw, sin_tw = turn_table(outer, inner, outer * inner, 1.0)
    turned_real = first_real * cos_tw + first_imag * sin_tw
    turned_imag = first_imag * cos_tw - first_real * sin_tw
    cos_in, sin_in = turn_table(inner, inner, inner, 1.0)
    spec_real = jnp.einsum("uckm,mj->uckj", turned_real, cos_in, precision=highest) + jnp.einsum(
        "uckm,mj->uckj", turned_imag, sin_in, precision=highest
    )
    spec_imag = jnp.einsum("uckm,mj->uckj", turned_imag, cos_in, precision=highest) - jnp.einsum(
        "uckm,mj->uckj", turned_real, sin_in, precision=highest
    )
    return spec_real, spec_imag


def inverse_dft(spec_real, spec_imag):
    count, chans, outer, inner = spec_real.shape
    cos_in, sin_in = turn_table(inner, inner, inner, 1.0)
    back_real = jnp.einsum("uckj,jm->uckm", spec_real, cos_in, precision=highest) - jnp.einsum(
        "uckj,jm->uckm", spec_imag, sin_in, precision=highest
    )
    back_imag = jnp.einsum("uckj,jm->uckm", spec_imag, cos_in, precision=highest) + jnp.einsum(
        "uckj,jm->uckm", spec_real, sin_in, precision=highest
    )
    cos_tw, sin_tw = turn_table(outer, inner, outer * inner, 1.0)
    turned_real = back_real * cos_tw - back_imag * sin_tw
    turned_imag = back_imag * cos_tw + back_real * sin_tw
    cos_out, sin_out = turn_table(outer, outer // 2, outer, 1.0)
    grid = jnp.einsum("kn,uckm->ucnm", cos_out, turned_real, precision=highest) - jnp.einsum(
        "kn,uckm->ucnm", sin_out, turned_imag, precision=highest
    )
    return grid.reshape(count, chans, outer * inner // 2) / float(outer * inner)


def per_device(
    inputs, norm_gain, in_weight, short_filter, long_filter, conv_bias, out_weight, out_grad
):
    local_rows = inputs.shape[0]
    model_width = inputs.shape[1]
    slab_width = long_filter.shape[1]
    taps = short_filter.shape[1]
    wide_inputs = inputs.astype(jnp.float32)
    inv_rms = lax.rsqrt(jnp.mean(wide_inputs * wide_inputs, axis=1, keepdims=True) + epsilon)
    normed = (wide_inputs * inv_rms * norm_gain).astype(jnp.bfloat16)
    in_panel, out_panel = (
        lax.all_gather(in_weight, "seq", axis=0, tiled=True),
        doubled_gather(out_weight.T, "seq").T,
    )
    in_flat = in_panel.reshape(model_width, 3 * slab_width)
    projected = jnp.dot(normed, in_flat, preferred_element_type=jnp.float32)
    projected = projected.astype(jnp.bfloat16).reshape(local_rows, 3, slab_width)
    upper_rim = passed_along(projected[local_rows - (taps - 1) :], "seq", 1)
    extended = jnp.concatenate([upper_rim, projected], 0).astype(jnp.float32)
    mixed = jnp.zeros((local_rows, 3, slab_width), jnp.float32)
    for offset in range(taps):
        begin = taps - 1 - offset
        mixed = mixed + short_filter[:, offset, :][None] * extended[begin : begin + local_rows]
    query_br = mixed[:, 0]
    key_br = mixed[:, 1]
    value_br = mixed[:, 2]
    product = key_br * value_br
    gate_grad = jnp.dot(out_grad, out_panel.T, preferred_element_type=jnp.float32)
    carried = gate_grad * query_br
    columns = to_columns(jnp.stack([product, long_filter, carried]).transpose(0, 2, 1))
    all_real, all_imag = forward_dft(columns)
    sig_real, filt_real, grad_real = (all_real[0], all_real[1], all_real[2])
    sig_imag, filt_imag, grad_imag = (all_imag[0], all_imag[1], all_imag[2])
    conv_real = sig_real * filt_real - sig_imag * filt_imag
    conv_imag = sig_real * filt_imag + sig_imag * filt_real
    back_real = grad_real * filt_real + grad_imag * filt_imag
    back_imag = grad_imag * filt_real - grad_real * filt_imag
    pair_real = grad_real * sig_real + grad_imag * sig_imag
    pair_imag = grad_imag * sig_real - grad_real * sig_imag
    outs = inverse_dft(
        jnp.stack([conv_real, back_real, pair_real]), jnp.stack([conv_imag, back_imag, pair_imag])
    )
    returned = to_rows(outs)
    conv_out = returned[0]
    back_conv = returned[1]
    filter_grad = returned[2] * float(local_rows * lax.axis_size("seq")) ** (-0.5)
    biased = conv_out + conv_bias * product
    gated = (query_br * biased).astype(jnp.bfloat16)
    partial_out = jnp.dot(gated, out_panel, preferred_element_type=jnp.float32)
    summed = lax.psum_scatter(
        partial_out.astype(jnp.bfloat16), "ch", scatter_dimension=1, tiled=True
    ).astype(jnp.float32)
    share = summed.shape[1]
    residual = lax.dynamic_slice_in_dim(wide_inputs, lax.axis_index("ch") * share, share, 1)
    block_out = (residual + summed).astype(jnp.bfloat16)
    source_grad = back_conv + conv_bias * carried
    mixed_grad = jnp.stack([gate_grad * biased, source_grad * value_br, source_grad * key_br], 1)
    lower_rim = passed_along(mixed_grad[: taps - 1], "seq", -1)
    extended_back = jnp.concatenate([mixed_grad, lower_rim], 0)
    proj_grad = jnp.zeros((local_rows, 3, slab_width), jnp.float32)
    for offset in range(taps):
        proj_grad = (
            proj_grad
            + short_filter[:, offset, :][None] * extended_back[offset : offset + local_rows]
        )
    proj_grad = proj_grad.astype(jnp.bfloat16).reshape(local_rows, 3 * slab_width)
    partial_grad = jnp.dot(proj_grad, in_flat.T, preferred_element_type=jnp.float32)
    norm_grad = lax.psum_scatter(
        partial_grad.astype(jnp.bfloat16), "ch", scatter_dimension=1, tiled=True
    ).astype(jnp.float32)
    feature_share = norm_grad.shape[1]
    feature_begin = lax.axis_index("ch") * feature_share
    gain_share = lax.dynamic_slice_in_dim(norm_gain, feature_begin, feature_share, 0)
    inputs_share = lax.dynamic_slice_in_dim(wide_inputs, feature_begin, feature_share, 1)
    grad_share = lax.dynamic_slice_in_dim(out_grad, feature_begin, feature_share, 1)
    weighted = norm_grad * gain_share
    inner_term = lax.psum(jnp.sum(weighted * inputs_share, axis=1, keepdims=True), "ch") / model_width
    in_grad_share = (
        grad_share.astype(jnp.float32) + weighted * inv_rms - inputs_share * inv_rms**3 * inner_term
    ).astype(jnp.bfloat16)
    in_grad = lax.all_gather(in_grad_share, "ch", axis=1, tiled=True)
    return (block_out, in_grad, filter_grad)


def solution(mesh):
    return jax.shard_map(
        per_device,
        mesh=mesh,
        in_specs=(
            P("seq", None),
            P(),
            P("seq", None, "ch"),
            P(None, None, "ch"),
            P("seq", "ch"),
            P("ch"),
            P("ch", "seq"),
            P("seq", None),
        ),
        out_specs=(P("seq", "ch"), P("seq", None), P("seq", "ch")),
        check_vma=False,
    )
```

```python
import math

import jax
import jax.numpy as jnp
from jax import lax
from jax.sharding import PartitionSpec as P

epsilon = 1e-05
highest = lax.Precision.HIGHEST


def passed_along(block, axis, distance):
    devices = range(lax.axis_size(axis))
    route = [(i - distance, i) for i in devices if i - distance in devices]
    return lax.ppermute(block, axis, route)


def doubled_gather(block, axis):
    devices = lax.axis_size(axis)
    place = lax.axis_index(axis)
    bits = devices.bit_length() - 1
    assert 1 << bits == devices
    gathered = block
    for bit in reversed(range(bits)):
        route = [(i, i ^ (1 << bit)) for i in range(devices)]
        arrived = lax.ppermute(gathered, axis, route)
        lower = ((place >> bit) & 1) == 0
        gathered = jnp.where(lower, jnp.stack([gathered, arrived]), jnp.stack([arrived, gathered]))
    gathered = gathered.transpose(tuple(reversed(range(bits))) + tuple(range(bits, gathered.ndim)))
    return gathered.reshape((devices * block.shape[0],) + block.shape[1:])


def halved_sum(partial, axis):
    devices = lax.axis_size(axis)
    place = lax.axis_index(axis)
    bits = devices.bit_length() - 1
    assert 1 << bits == devices
    rows, width = partial.shape
    share = width // devices
    held = partial.reshape((rows,) + (2,) * bits + (share,))
    held = held.astype(jnp.float32)
    for bit in reversed(range(bits)):
        route = [(i, i ^ (1 << bit)) for i in range(devices)]
        mine = (place >> bit) & 1
        kept = lax.dynamic_index_in_dim(held, mine, 1, keepdims=False)
        given = lax.dynamic_index_in_dim(held, 1 - mine, 1, keepdims=False)
        arrived = lax.ppermute(given.astype(jnp.bfloat16), axis, route)
        held = kept + arrived.astype(jnp.float32)
    return held


def to_columns(signals):
    return lax.all_to_all(signals, "seq", split_axis=1, concat_axis=2, tiled=True)


def to_rows(signals):
    count, chans, seq_total = signals.shape
    devices = lax.axis_size("seq")
    local_rows = seq_total // devices
    pieces = signals.reshape(count, chans, devices, local_rows).transpose(2, 0, 1, 3)
    arrived = lax.all_to_all(pieces, "seq", split_axis=0, concat_axis=0, tiled=True)
    return arrived.transpose(1, 3, 0, 2).reshape(count, local_rows, devices * chans)


def turn_table(rows, cols, period, sign):
    turns = jnp.arange(rows, dtype=jnp.int32)[:, None] * jnp.arange(cols, dtype=jnp.int32)[None, :]
    phases = sign * 2.0 * math.pi / period * (turns % period).astype(jnp.float32)
    return (jnp.cos(phases), jnp.sin(phases))


def fft_sizes(seq_total):
    total = 2 * seq_total
    inner = 1
    while inner * inner < total:
        inner *= 2
    return total // inner, inner


def forward_dft(signals):
    count, chans, seq_total = signals.shape
    outer, inner = fft_sizes(seq_total)
    grid = signals.reshape(count, chans, outer // 2, inner)
    cos_out, sin_out = turn_table(outer, outer // 2, outer, 1.0)
    first_real = jnp.einsum("kn,ucnm->uckm", cos_out, grid, precision=highest)
    first_imag = -jnp.einsum("kn,ucnm->uckm", sin_out, grid, precision=highest)
    cos_tw, sin_tw = turn_table(outer, inner, outer * inner, 1.0)
    turned_real = first_real * cos_tw + first_imag * sin_tw
    turned_imag = first_imag * cos_tw - first_real * sin_tw
    cos_in, sin_in = turn_table(inner, inner, inner, 1.0)
    spec_real = jnp.einsum("uckm,mj->uckj", turned_real, cos_in, precision=highest) + jnp.einsum(
        "uckm,mj->uckj", turned_imag, sin_in, precision=highest
    )
    spec_imag = jnp.einsum("uckm,mj->uckj", turned_imag, cos_in, precision=highest) - jnp.einsum(
        "uckm,mj->uckj", turned_real, sin_in, precision=highest
    )
    return spec_real, spec_imag


def inverse_dft(spec_real, spec_imag):
    count, chans, outer, inner = spec_real.shape
    cos_in, sin_in = turn_table(inner, inner, inner, 1.0)
    back_real = jnp.einsum("uckj,jm->uckm", spec_real, cos_in, precision=highest) - jnp.einsum(
        "uckj,jm->uckm", spec_imag, sin_in, precision=highest
    )
    back_imag = jnp.einsum("uckj,jm->uckm", spec_imag, cos_in, precision=highest) + jnp.einsum(
        "uckj,jm->uckm", spec_real, sin_in, precision=highest
    )
    cos_tw, sin_tw = turn_table(outer, inner, outer * inner, 1.0)
    turned_real = back_real * cos_tw - back_imag * sin_tw
    turned_imag = back_imag * cos_tw + back_real * sin_tw
    cos_out, sin_out = turn_table(outer, outer // 2, outer, 1.0)
    grid = jnp.einsum("kn,uckm->ucnm", cos_out, turned_real, precision=highest) - jnp.einsum(
        "kn,uckm->ucnm", sin_out, turned_imag, precision=highest
    )
    return grid.reshape(count, chans, outer * inner // 2) / float(outer * inner)


def per_device(
    inputs, norm_gain, in_weight, short_filter, long_filter, conv_bias, out_weight, out_grad
):
    local_rows = inputs.shape[0]
    model_width = inputs.shape[1]
    slab_width = long_filter.shape[1]
    taps = short_filter.shape[1]
    wide_inputs = inputs.astype(jnp.float32)
    inv_rms = lax.rsqrt(jnp.mean(wide_inputs * wide_inputs, axis=1, keepdims=True) + epsilon)
    normed = (wide_inputs * inv_rms * norm_gain).astype(jnp.bfloat16)
    in_panel, out_panel = (
        lax.all_gather(in_weight, "seq", axis=0, tiled=True),
        doubled_gather(out_weight.T, "seq").T,
    )
    in_flat = in_panel.reshape(model_width, 3 * slab_width)
    projected = jnp.dot(normed, in_flat, preferred_element_type=jnp.float32)
    projected = projected.astype(jnp.bfloat16).reshape(local_rows, 3, slab_width)
    upper_rim = passed_along(projected[local_rows - (taps - 1) :], "seq", 1)
    extended = jnp.concatenate([upper_rim, projected], 0).astype(jnp.float32)
    mixed = jnp.zeros((local_rows, 3, slab_width), jnp.float32)
    for offset in range(taps):
        begin = taps - 1 - offset
        mixed = mixed + short_filter[:, offset, :][None] * extended[begin : begin + local_rows]
    query_br = mixed[:, 0]
    key_br = mixed[:, 1]
    value_br = mixed[:, 2]
    product = key_br * value_br
    gate_grad = jnp.dot(out_grad, out_panel.T, preferred_element_type=jnp.float32)
    carried = gate_grad * query_br
    columns = to_columns(jnp.stack([product, long_filter, carried]).transpose(0, 2, 1))
    all_real, all_imag = forward_dft(columns)
    sig_real, filt_real, grad_real = (all_real[0], all_real[1], all_real[2])
    sig_imag, filt_imag, grad_imag = (all_imag[0], all_imag[1], all_imag[2])
    conv_real = sig_real * filt_real - sig_imag * filt_imag
    conv_imag = sig_real * filt_imag + sig_imag * filt_real
    back_real = grad_real * filt_real + grad_imag * filt_imag
    back_imag = grad_imag * filt_real - grad_real * filt_imag
    pair_real = grad_real * sig_real + grad_imag * sig_imag
    pair_imag = grad_imag * sig_real - grad_real * sig_imag
    outs = inverse_dft(
        jnp.stack([conv_real, back_real, pair_real]), jnp.stack([conv_imag, back_imag, pair_imag])
    )
    returned = to_rows(outs)
    conv_out = returned[0]
    back_conv = returned[1]
    filter_grad = returned[2] * float(local_rows * lax.axis_size("seq")) ** (-0.5)
    biased = conv_out + conv_bias * product
    gated = (query_br * biased).astype(jnp.bfloat16)
    partial_out = jnp.dot(gated, out_panel, preferred_element_type=jnp.float32)
    summed = halved_sum(partial_out.astype(jnp.bfloat16), "ch")
    share = summed.shape[1]
    residual = lax.dynamic_slice_in_dim(wide_inputs, lax.axis_index("ch") * share, share, 1)
    block_out = (residual + summed).astype(jnp.bfloat16)
    source_grad = back_conv + conv_bias * carried
    mixed_grad = jnp.stack([gate_grad * biased, source_grad * value_br, source_grad * key_br], 1)
    lower_rim = passed_along(mixed_grad[: taps - 1], "seq", -1)
    extended_back = jnp.concatenate([mixed_grad, lower_rim], 0)
    proj_grad = jnp.zeros((local_rows, 3, slab_width), jnp.float32)
    for offset in range(taps):
        proj_grad = (
            proj_grad
            + short_filter[:, offset, :][None] * extended_back[offset : offset + local_rows]
        )
    proj_grad = proj_grad.astype(jnp.bfloat16).reshape(local_rows, 3 * slab_width)
    partial_grad = jnp.dot(proj_grad, in_flat.T, preferred_element_type=jnp.float32)
    ch_size = lax.axis_size("ch")
    feature_share = model_width // ch_size
    partial_inner = jnp.sum(partial_grad * (norm_gain * wide_inputs), axis=1, keepdims=True)
    inner_high = partial_inner.astype(jnp.bfloat16)
    inner_low = (partial_inner - inner_high.astype(jnp.float32)).astype(jnp.bfloat16)
    extra = jnp.concatenate(
        [inner_high, inner_low, jnp.zeros((local_rows, 126), jnp.bfloat16)], axis=1
    )
    payload = jnp.concatenate(
        [
            partial_grad.astype(jnp.bfloat16).reshape(local_rows, ch_size, feature_share),
            jnp.broadcast_to(extra[:, None, :], (local_rows, ch_size, 128)),
        ],
        axis=2,
    ).reshape(local_rows, ch_size * (feature_share + 128))
    reduced = lax.psum_scatter(payload, "ch", scatter_dimension=1, tiled=True).astype(jnp.float32)
    norm_grad = reduced[:, :feature_share]
    inner_term = (reduced[:, feature_share : feature_share + 1] + reduced[:, feature_share + 1 : feature_share + 2]) / model_width
    feature_begin = lax.axis_index("ch") * feature_share
    gain_share = lax.dynamic_slice_in_dim(norm_gain, feature_begin, feature_share, 0)
    inputs_share = lax.dynamic_slice_in_dim(wide_inputs, feature_begin, feature_share, 1)
    grad_share = lax.dynamic_slice_in_dim(out_grad, feature_begin, feature_share, 1)
    weighted = norm_grad * gain_share
    in_grad_share = (
        grad_share.astype(jnp.float32) + weighted * inv_rms - inputs_share * inv_rms**3 * inner_term
    ).astype(jnp.bfloat16)
    in_grad = lax.all_gather(in_grad_share, "ch", axis=1, tiled=True)
    return (block_out, in_grad, filter_grad)


def solution(mesh):
    return jax.shard_map(
        per_device,
        mesh=mesh,
        in_specs=(
            P("seq", None),
            P(),
            P("seq", None, "ch"),
            P(None, None, "ch"),
            P("seq", "ch"),
            P("ch"),
            P("ch", "seq"),
            P("seq", None),
        ),
        out_specs=(P("seq", "ch"), P("seq", None), P("seq", "ch")),
        check_vma=False,
    )
```

```python
import math

import jax
import jax.numpy as jnp
from jax import lax
from jax.sharding import PartitionSpec as P

epsilon = 1e-05
highest = lax.Precision.HIGHEST


def passed_along(block, axis, distance):
    devices = range(lax.axis_size(axis))
    route = [(i - distance, i) for i in devices if i - distance in devices]
    return lax.ppermute(block, axis, route)


def doubled_gather(block, axis):
    devices = lax.axis_size(axis)
    place = lax.axis_index(axis)
    bits = devices.bit_length() - 1
    assert 1 << bits == devices
    gathered = block
    for bit in reversed(range(bits)):
        route = [(i, i ^ (1 << bit)) for i in range(devices)]
        arrived = lax.ppermute(gathered, axis, route)
        lower = ((place >> bit) & 1) == 0
        gathered = jnp.where(lower, jnp.stack([gathered, arrived]), jnp.stack([arrived, gathered]))
    gathered = gathered.transpose(tuple(reversed(range(bits))) + tuple(range(bits, gathered.ndim)))
    return gathered.reshape((devices * block.shape[0],) + block.shape[1:])


def halved_sum(partial, axis):
    devices = lax.axis_size(axis)
    place = lax.axis_index(axis)
    bits = devices.bit_length() - 1
    assert 1 << bits == devices
    rows, width = partial.shape
    share = width // devices
    held = partial.reshape((rows,) + (2,) * bits + (share,))
    held = held.transpose((0,) + tuple(range(bits, 0, -1)) + (bits + 1,)).astype(jnp.float32)
    for bit in range(bits):
        route = [(i, i ^ (1 << bit)) for i in range(devices)]
        mine = (place >> bit) & 1
        kept = lax.dynamic_index_in_dim(held, mine, 1, keepdims=False)
        given = lax.dynamic_index_in_dim(held, 1 - mine, 1, keepdims=False)
        arrived = lax.ppermute(given.astype(jnp.bfloat16), axis, route)
        held = kept + arrived.astype(jnp.float32)
    return held


def to_columns(signals):
    return lax.all_to_all(signals, "seq", split_axis=1, concat_axis=2, tiled=True)


def to_rows(signals):
    count, chans, seq_total = signals.shape
    devices = lax.axis_size("seq")
    local_rows = seq_total // devices
    pieces = signals.reshape(count, chans, devices, local_rows).transpose(2, 0, 1, 3)
    arrived = lax.all_to_all(pieces, "seq", split_axis=0, concat_axis=0, tiled=True)
    return arrived.transpose(1, 3, 0, 2).reshape(count, local_rows, devices * chans)


def turn_table(rows, cols, period, sign):
    turns = jnp.arange(rows, dtype=jnp.int32)[:, None] * jnp.arange(cols, dtype=jnp.int32)[None, :]
    turns = lax.optimization_barrier(turns)
    phases = sign * 2.0 * math.pi / period * (turns % period).astype(jnp.float32)
    return (jnp.cos(phases), jnp.sin(phases))


def fft_sizes(seq_total):
    total = 2 * seq_total
    inner = 1
    while inner * inner < total:
        inner *= 2
    return total // inner, inner


def forward_dft(signals):
    count, chans, seq_total = signals.shape
    outer, inner = fft_sizes(seq_total)
    grid = signals.reshape(count, chans, outer // 2, inner)
    cos_out, sin_out = turn_table(outer, outer // 2, outer, 1.0)
    first_real = jnp.einsum("kn,ucnm->uckm", cos_out, grid, precision=highest)
    first_imag = -jnp.einsum("kn,ucnm->uckm", sin_out, grid, precision=highest)
    cos_tw, sin_tw = turn_table(outer, inner, outer * inner, 1.0)
    turned_real = first_real * cos_tw + first_imag * sin_tw
    turned_imag = first_imag * cos_tw - first_real * sin_tw
    cos_in, sin_in = turn_table(inner, inner, inner, 1.0)
    spec_real = jnp.einsum("uckm,mj->uckj", turned_real, cos_in, precision=highest) + jnp.einsum(
        "uckm,mj->uckj", turned_imag, sin_in, precision=highest
    )
    spec_imag = jnp.einsum("uckm,mj->uckj", turned_imag, cos_in, precision=highest) - jnp.einsum(
        "uckm,mj->uckj", turned_real, sin_in, precision=highest
    )
    return spec_real, spec_imag


def inverse_dft(spec_real, spec_imag):
    count, chans, outer, inner = spec_real.shape
    cos_in, sin_in = turn_table(inner, inner, inner, 1.0)
    back_real = jnp.einsum("uckj,jm->uckm", spec_real, cos_in, precision=highest) - jnp.einsum(
        "uckj,jm->uckm", spec_imag, sin_in, precision=highest
    )
    back_imag = jnp.einsum("uckj,jm->uckm", spec_imag, cos_in, precision=highest) + jnp.einsum(
        "uckj,jm->uckm", spec_real, sin_in, precision=highest
    )
    cos_tw, sin_tw = turn_table(outer, inner, outer * inner, 1.0)
    turned_real = back_real * cos_tw - back_imag * sin_tw
    turned_imag = back_imag * cos_tw + back_real * sin_tw
    cos_out, sin_out = turn_table(outer, outer // 2, outer, 1.0)
    grid = jnp.einsum("kn,uckm->ucnm", cos_out, turned_real, precision=highest) - jnp.einsum(
        "kn,uckm->ucnm", sin_out, turned_imag, precision=highest
    )
    return grid.reshape(count, chans, outer * inner // 2) / float(outer * inner)


def per_device(
    inputs, norm_gain, in_weight, short_filter, long_filter, conv_bias, out_weight, out_grad
):
    local_rows = inputs.shape[0]
    model_width = inputs.shape[1]
    slab_width = long_filter.shape[1]
    taps = short_filter.shape[1]
    wide_inputs = inputs.astype(jnp.float32)
    inv_rms = lax.rsqrt(jnp.mean(wide_inputs * wide_inputs, axis=1, keepdims=True) + epsilon)
    normed = (wide_inputs * inv_rms * norm_gain).astype(jnp.bfloat16)
    in_panel, out_panel = (
        lax.all_gather(in_weight, "seq", axis=0, tiled=True),
        doubled_gather(out_weight.T, "seq").T,
    )
    in_flat = in_panel.reshape(model_width, 3 * slab_width)
    projected = jnp.dot(normed, in_flat, preferred_element_type=jnp.float32)
    projected = projected.astype(jnp.bfloat16).reshape(local_rows, 3, slab_width)
    upper_rim = passed_along(projected[local_rows - (taps - 1) :], "seq", 1)
    extended = jnp.concatenate([upper_rim, projected], 0).astype(jnp.float32)
    mixed = jnp.zeros((local_rows, 3, slab_width), jnp.float32)
    for offset in range(taps):
        begin = taps - 1 - offset
        mixed = mixed + short_filter[:, offset, :][None] * extended[begin : begin + local_rows]
    query_br = mixed[:, 0]
    key_br = mixed[:, 1]
    value_br = mixed[:, 2]
    product = key_br * value_br
    gate_grad = jnp.dot(out_grad, out_panel.T, preferred_element_type=jnp.float32)
    carried = gate_grad * query_br
    columns = to_columns(jnp.stack([product, long_filter, carried]).transpose(0, 2, 1))
    all_real, all_imag = forward_dft(columns)
    sig_real, filt_real, grad_real = (all_real[0], all_real[1], all_real[2])
    sig_imag, filt_imag, grad_imag = (all_imag[0], all_imag[1], all_imag[2])
    conv_real = sig_real * filt_real - sig_imag * filt_imag
    conv_imag = sig_real * filt_imag + sig_imag * filt_real
    back_real = grad_real * filt_real + grad_imag * filt_imag
    back_imag = grad_imag * filt_real - grad_real * filt_imag
    pair_real = grad_real * sig_real + grad_imag * sig_imag
    pair_imag = grad_imag * sig_real - grad_real * sig_imag
    outs = inverse_dft(
        jnp.stack([conv_real, back_real, pair_real]), jnp.stack([conv_imag, back_imag, pair_imag])
    )
    returned = to_rows(outs)
    conv_out = returned[0]
    back_conv = returned[1]
    filter_grad = returned[2] * float(local_rows * lax.axis_size("seq")) ** (-0.5)
    biased = conv_out + conv_bias * product
    gated = (query_br * biased).astype(jnp.bfloat16)
    partial_out = jnp.dot(gated, out_panel, preferred_element_type=jnp.float32)
    summed = halved_sum(partial_out.astype(jnp.bfloat16), "ch")
    share = summed.shape[1]
    residual = lax.dynamic_slice_in_dim(wide_inputs, lax.axis_index("ch") * share, share, 1)
    block_out = (residual + summed).astype(jnp.bfloat16)
    source_grad = back_conv + conv_bias * carried
    mixed_grad = jnp.stack([gate_grad * biased, source_grad * value_br, source_grad * key_br], 1)
    lower_rim = passed_along(mixed_grad[: taps - 1], "seq", -1)
    extended_back = jnp.concatenate([mixed_grad, lower_rim], 0)
    proj_grad = jnp.zeros((local_rows, 3, slab_width), jnp.float32)
    for offset in range(taps):
        proj_grad = (
            proj_grad
            + short_filter[:, offset, :][None] * extended_back[offset : offset + local_rows]
        )
    proj_grad = proj_grad.astype(jnp.bfloat16).reshape(local_rows, 3 * slab_width)
    partial_grad = jnp.dot(proj_grad, in_flat.T, preferred_element_type=jnp.float32)
    ch_size = lax.axis_size("ch")
    feature_share = model_width // ch_size
    partial_inner = jnp.sum(partial_grad * (norm_gain * wide_inputs), axis=1, keepdims=True)
    inner_high = partial_inner.astype(jnp.bfloat16)
    inner_low = (partial_inner - inner_high.astype(jnp.float32)).astype(jnp.bfloat16)
    extra = jnp.concatenate(
        [inner_high, inner_low, jnp.zeros((local_rows, 126), jnp.bfloat16)], axis=1
    )
    payload = jnp.concatenate(
        [
            partial_grad.astype(jnp.bfloat16).reshape(local_rows, ch_size, feature_share),
            jnp.broadcast_to(extra[:, None, :], (local_rows, ch_size, 128)),
        ],
        axis=2,
    ).reshape(local_rows, ch_size * (feature_share + 128))
    reduced = lax.psum_scatter(payload, "ch", scatter_dimension=1, tiled=True).astype(jnp.float32)
    norm_grad = reduced[:, :feature_share]
    inner_term = (reduced[:, feature_share : feature_share + 1] + reduced[:, feature_share + 1 : feature_share + 2]) / model_width
    feature_begin = lax.axis_index("ch") * feature_share
    gain_share = lax.dynamic_slice_in_dim(norm_gain, feature_begin, feature_share, 0)
    inputs_share = lax.dynamic_slice_in_dim(wide_inputs, feature_begin, feature_share, 1)
    grad_share = lax.dynamic_slice_in_dim(out_grad, feature_begin, feature_share, 1)
    weighted = norm_grad * gain_share
    in_grad_share = (
        grad_share.astype(jnp.float32) + weighted * inv_rms - inputs_share * inv_rms**3 * inner_term
    ).astype(jnp.bfloat16)
    in_grad = doubled_gather(in_grad_share[None], "ch").transpose(1, 0, 2).reshape(local_rows, model_width)
    return (block_out, in_grad, filter_grad)


def solution(mesh):
    return jax.shard_map(
        per_device,
        mesh=mesh,
        in_specs=(
            P("seq", None),
            P(),
            P("seq", None, "ch"),
            P(None, None, "ch"),
            P("seq", "ch"),
            P("ch"),
            P("ch", "seq"),
            P("seq", None),
        ),
        out_specs=(P("seq", "ch"), P("seq", None), P("seq", "ch")),
        check_vma=False,
    )
```

```python
import math

import jax
import jax.numpy as jnp
from jax import lax
from jax.sharding import PartitionSpec as P

epsilon = 1e-05
highest = lax.Precision.HIGHEST


def passed_along(block, axis, distance):
    devices = range(lax.axis_size(axis))
    route = [(i - distance, i) for i in devices if i - distance in devices]
    return lax.ppermute(block, axis, route)


def doubled_gather(block, axis):
    devices = lax.axis_size(axis)
    place = lax.axis_index(axis)
    bits = devices.bit_length() - 1
    assert 1 << bits == devices
    gathered = block
    for bit in reversed(range(bits)):
        route = [(i, i ^ (1 << bit)) for i in range(devices)]
        arrived = lax.ppermute(gathered, axis, route)
        lower = ((place >> bit) & 1) == 0
        gathered = jnp.where(lower, jnp.stack([gathered, arrived]), jnp.stack([arrived, gathered]))
    gathered = gathered.transpose(tuple(reversed(range(bits))) + tuple(range(bits, gathered.ndim)))
    return gathered.reshape((devices * block.shape[0],) + block.shape[1:])


def halved_sum(partial, axis):
    devices = lax.axis_size(axis)
    place = lax.axis_index(axis)
    bits = devices.bit_length() - 1
    assert 1 << bits == devices
    rows, width = partial.shape
    share = width // devices
    held = partial.reshape((rows,) + (2,) * bits + (share,))
    held = held.transpose((0,) + tuple(range(bits, 0, -1)) + (bits + 1,)).astype(jnp.float32)
    for bit in range(bits):
        route = [(i, i ^ (1 << bit)) for i in range(devices)]
        mine = (place >> bit) & 1
        kept = lax.dynamic_index_in_dim(held, mine, 1, keepdims=False)
        given = lax.dynamic_index_in_dim(held, 1 - mine, 1, keepdims=False)
        arrived = lax.ppermute(given.astype(jnp.bfloat16), axis, route)
        held = kept + arrived.astype(jnp.float32)
    return held


def to_columns(signals):
    return lax.all_to_all(signals, "seq", split_axis=1, concat_axis=2, tiled=True)


def to_rows(signals):
    count, chans, seq_total = signals.shape
    devices = lax.axis_size("seq")
    local_rows = seq_total // devices
    pieces = signals.reshape(count, chans, devices, local_rows).transpose(2, 0, 1, 3)
    arrived = lax.all_to_all(pieces, "seq", split_axis=0, concat_axis=0, tiled=True)
    return arrived.transpose(1, 3, 0, 2).reshape(count, local_rows, devices * chans)


def turn_table(rows, cols, period, sign):
    turns = jnp.arange(rows, dtype=jnp.int32)[:, None] * jnp.arange(cols, dtype=jnp.int32)[None, :]
    turns = lax.optimization_barrier(turns)
    phases = sign * 2.0 * math.pi / period * (turns % period).astype(jnp.float32)
    return (jnp.cos(phases), jnp.sin(phases))


def fft_sizes(seq_total):
    total = 2 * seq_total
    inner = 1
    while inner * inner < total:
        inner *= 2
    return total // inner, inner


def forward_dft(signals):
    count, chans, seq_total = signals.shape
    outer, inner = fft_sizes(seq_total)
    grid = signals.reshape(count, chans, outer // 2, inner)
    cos_out, sin_out = turn_table(outer, outer // 2, outer, 1.0)
    first_real = jnp.einsum("kn,ucnm->uckm", cos_out, grid, precision=highest)
    first_imag = -jnp.einsum("kn,ucnm->uckm", sin_out, grid, precision=highest)
    cos_tw, sin_tw = turn_table(outer, inner, outer * inner, 1.0)
    turned_real = first_real * cos_tw + first_imag * sin_tw
    turned_imag = first_imag * cos_tw - first_real * sin_tw
    cos_in, sin_in = turn_table(inner, inner, inner, 1.0)
    spec_real = jnp.einsum("uckm,mj->uckj", turned_real, cos_in, precision=highest) + jnp.einsum(
        "uckm,mj->uckj", turned_imag, sin_in, precision=highest
    )
    spec_imag = jnp.einsum("uckm,mj->uckj", turned_imag, cos_in, precision=highest) - jnp.einsum(
        "uckm,mj->uckj", turned_real, sin_in, precision=highest
    )
    return spec_real, spec_imag


def inverse_dft(spec_real, spec_imag):
    count, chans, outer, inner = spec_real.shape
    cos_in, sin_in = turn_table(inner, inner, inner, 1.0)
    back_real = jnp.einsum("uckj,jm->uckm", spec_real, cos_in, precision=highest) - jnp.einsum(
        "uckj,jm->uckm", spec_imag, sin_in, precision=highest
    )
    back_imag = jnp.einsum("uckj,jm->uckm", spec_imag, cos_in, precision=highest) + jnp.einsum(
        "uckj,jm->uckm", spec_real, sin_in, precision=highest
    )
    cos_tw, sin_tw = turn_table(outer, inner, outer * inner, 1.0)
    turned_real = back_real * cos_tw - back_imag * sin_tw
    turned_imag = back_imag * cos_tw + back_real * sin_tw
    cos_out, sin_out = turn_table(outer, outer // 2, outer, 1.0)
    grid = jnp.einsum("kn,uckm->ucnm", cos_out, turned_real, precision=highest) - jnp.einsum(
        "kn,uckm->ucnm", sin_out, turned_imag, precision=highest
    )
    return grid.reshape(count, chans, outer * inner // 2) / float(outer * inner)


def per_device(
    inputs, norm_gain, in_weight, short_filter, long_filter, conv_bias, out_weight, out_grad
):
    local_rows = inputs.shape[0]
    model_width = inputs.shape[1]
    slab_width = long_filter.shape[1]
    taps = short_filter.shape[1]
    wide_inputs = inputs.astype(jnp.float32)
    inv_rms = lax.rsqrt(jnp.mean(wide_inputs * wide_inputs, axis=1, keepdims=True) + epsilon)
    normed = (wide_inputs * inv_rms * norm_gain).astype(jnp.bfloat16)
    in_panel, out_panel = (
        lax.all_gather(in_weight, "seq", axis=0, tiled=True),
        doubled_gather(out_weight.T, "seq").T,
    )
    in_flat = in_panel.reshape(model_width, 3 * slab_width)
    projected = jnp.dot(normed, in_flat, preferred_element_type=jnp.float32)
    projected = projected.astype(jnp.bfloat16).reshape(local_rows, 3, slab_width)
    upper_rim = passed_along(projected[local_rows - (taps - 1) :], "seq", 1)
    extended = jnp.concatenate([upper_rim, projected], 0).astype(jnp.float32)
    mixed = jnp.zeros((local_rows, 3, slab_width), jnp.float32)
    for offset in range(taps):
        begin = taps - 1 - offset
        mixed = mixed + short_filter[:, offset, :][None] * extended[begin : begin + local_rows]
    query_br = mixed[:, 0]
    key_br = mixed[:, 1]
    value_br = mixed[:, 2]
    product = key_br * value_br
    gate_grad = jnp.dot(out_grad, out_panel.T, preferred_element_type=jnp.float32)
    carried = gate_grad * query_br
    columns = to_columns(jnp.stack([product, long_filter, carried]).transpose(0, 2, 1))
    all_real, all_imag = forward_dft(columns)
    sig_real, filt_real, grad_real = (all_real[0], all_real[1], all_real[2])
    sig_imag, filt_imag, grad_imag = (all_imag[0], all_imag[1], all_imag[2])
    conv_real = sig_real * filt_real - sig_imag * filt_imag
    conv_imag = sig_real * filt_imag + sig_imag * filt_real
    back_real = grad_real * filt_real + grad_imag * filt_imag
    back_imag = grad_imag * filt_real - grad_real * filt_imag
    pair_real = grad_real * sig_real + grad_imag * sig_imag
    pair_imag = grad_imag * sig_real - grad_real * sig_imag
    outs = inverse_dft(
        jnp.stack([conv_real, back_real, pair_real]), jnp.stack([conv_imag, back_imag, pair_imag])
    )
    returned = to_rows(outs)
    conv_out = returned[0]
    back_conv = returned[1]
    filter_grad = returned[2] * float(local_rows * lax.axis_size("seq")) ** (-0.5)
    biased = conv_out + conv_bias * product
    gated = (query_br * biased).astype(jnp.bfloat16)
    partial_out = jnp.dot(gated, out_panel, preferred_element_type=jnp.float32)
    summed = halved_sum(partial_out.astype(jnp.bfloat16), "ch")
    share = summed.shape[1]
    residual = lax.dynamic_slice_in_dim(wide_inputs, lax.axis_index("ch") * share, share, 1)
    block_out = (residual + summed).astype(jnp.bfloat16)
    source_grad = back_conv + conv_bias * carried
    mixed_grad = jnp.stack([gate_grad * biased, source_grad * value_br, source_grad * key_br], 1)
    lower_rim = passed_along(mixed_grad[: taps - 1], "seq", -1)
    extended_back = jnp.concatenate([mixed_grad, lower_rim], 0)
    proj_grad = jnp.zeros((local_rows, 3, slab_width), jnp.float32)
    for offset in range(taps):
        proj_grad = (
            proj_grad
            + short_filter[:, offset, :][None] * extended_back[offset : offset + local_rows]
        )
    proj_grad = proj_grad.astype(jnp.bfloat16).reshape(local_rows, 3 * slab_width)
    partial_grad = jnp.dot(proj_grad, in_flat.T, preferred_element_type=jnp.float32)
    ch_size = lax.axis_size("ch")
    feature_share = model_width // ch_size
    partial_inner = jnp.sum(partial_grad * (norm_gain * wide_inputs), axis=1, keepdims=True)
    inner_high = partial_inner.astype(jnp.bfloat16)
    inner_low = (partial_inner - inner_high.astype(jnp.float32)).astype(jnp.bfloat16)
    extra = jnp.concatenate(
        [inner_high, inner_low, jnp.zeros((local_rows, 126), jnp.bfloat16)], axis=1
    )
    payload = jnp.concatenate(
        [
            partial_grad.astype(jnp.bfloat16).reshape(local_rows, ch_size, feature_share).transpose(1, 0, 2),
            jnp.broadcast_to(extra[None], (ch_size, local_rows, 128)),
        ],
        axis=2,
    )
    reduced = lax.psum_scatter(payload, "ch", scatter_dimension=0).astype(jnp.float32)
    norm_grad = reduced[:, :feature_share]
    inner_term = (reduced[:, feature_share : feature_share + 1] + reduced[:, feature_share + 1 : feature_share + 2]) / model_width
    feature_begin = lax.axis_index("ch") * feature_share
    gain_share = lax.dynamic_slice_in_dim(norm_gain, feature_begin, feature_share, 0)
    inputs_share = lax.dynamic_slice_in_dim(wide_inputs, feature_begin, feature_share, 1)
    grad_share = lax.dynamic_slice_in_dim(out_grad, feature_begin, feature_share, 1)
    weighted = norm_grad * gain_share
    in_grad_share = (
        grad_share.astype(jnp.float32) + weighted * inv_rms - inputs_share * inv_rms**3 * inner_term
    ).astype(jnp.bfloat16)
    in_grad = doubled_gather(in_grad_share[None], "ch").transpose(1, 0, 2).reshape(local_rows, model_width)
    return (block_out, in_grad, filter_grad)


def solution(mesh):
    return jax.shard_map(
        per_device,
        mesh=mesh,
        in_specs=(
            P("seq", None),
            P(),
            P("seq", None, "ch"),
            P(None, None, "ch"),
            P("seq", "ch"),
            P("ch"),
            P("ch", "seq"),
            P("seq", None),
        ),
        out_specs=(P("seq", "ch"), P("seq", None), P("seq", "ch")),
        check_vma=False,
    )
```

```python
import math

import jax
import jax.numpy as jnp
from jax import lax
from jax.sharding import PartitionSpec as P

epsilon = 1e-05
highest = lax.Precision.HIGHEST


def passed_along(block, axis, distance):
    devices = range(lax.axis_size(axis))
    route = [(i - distance, i) for i in devices if i - distance in devices]
    return lax.ppermute(block, axis, route)


def doubled_gather(block, axis):
    devices = lax.axis_size(axis)
    place = lax.axis_index(axis)
    bits = devices.bit_length() - 1
    assert 1 << bits == devices
    gathered = block
    for bit in reversed(range(bits)):
        route = [(i, i ^ (1 << bit)) for i in range(devices)]
        arrived = lax.ppermute(gathered, axis, route)
        lower = ((place >> bit) & 1) == 0
        gathered = jnp.where(lower, jnp.stack([gathered, arrived]), jnp.stack([arrived, gathered]))
    gathered = gathered.transpose(tuple(reversed(range(bits))) + tuple(range(bits, gathered.ndim)))
    return gathered.reshape((devices * block.shape[0],) + block.shape[1:])


def halved_sum(partial, axis):
    devices = lax.axis_size(axis)
    place = lax.axis_index(axis)
    bits = devices.bit_length() - 1
    assert 1 << bits == devices
    rows, width = partial.shape
    share = width // devices
    held = partial.reshape((rows,) + (2,) * bits + (share,))
    held = held.transpose((0,) + tuple(range(bits, 0, -1)) + (bits + 1,)).astype(jnp.float32)
    for bit in range(bits):
        route = [(i, i ^ (1 << bit)) for i in range(devices)]
        mine = (place >> bit) & 1
        kept = lax.dynamic_index_in_dim(held, mine, 1, keepdims=False)
        given = lax.dynamic_index_in_dim(held, 1 - mine, 1, keepdims=False)
        arrived = lax.ppermute(given.astype(jnp.bfloat16), axis, route)
        held = kept + arrived.astype(jnp.float32)
    return held


def to_columns(signals):
    return lax.all_to_all(signals, "seq", split_axis=1, concat_axis=2, tiled=True)


def to_rows(signals):
    count, chans, seq_total = signals.shape
    devices = lax.axis_size("seq")
    local_rows = seq_total // devices
    pieces = signals.reshape(count, chans, devices, local_rows).transpose(2, 0, 1, 3)
    arrived = lax.all_to_all(pieces, "seq", split_axis=0, concat_axis=0, tiled=True)
    return arrived.transpose(1, 3, 0, 2).reshape(count, local_rows, devices * chans)


def turn_table(rows, cols, period, sign):
    turns = jnp.arange(rows, dtype=jnp.int32)[:, None] * jnp.arange(cols, dtype=jnp.int32)[None, :]
    turns = lax.optimization_barrier(turns)
    phases = sign * 2.0 * math.pi / period * (turns % period).astype(jnp.float32)
    return (jnp.cos(phases), jnp.sin(phases))


def fft_sizes(seq_total):
    total = 2 * seq_total
    inner = 1
    while inner * inner < total:
        inner *= 2
    return total // inner, inner


def forward_dft(signals):
    count, chans, seq_total = signals.shape
    outer, inner = fft_sizes(seq_total)
    grid = signals.reshape(count, chans, outer // 2, inner)
    cos_out, sin_out = turn_table(outer, outer // 2, outer, 1.0)
    first_real = jnp.einsum("kn,ucnm->uckm", cos_out, grid, precision=highest)
    first_imag = -jnp.einsum("kn,ucnm->uckm", sin_out, grid, precision=highest)
    cos_tw, sin_tw = turn_table(outer, inner, outer * inner, 1.0)
    turned_real = first_real * cos_tw + first_imag * sin_tw
    turned_imag = first_imag * cos_tw - first_real * sin_tw
    cos_in, sin_in = turn_table(inner, inner, inner, 1.0)
    spec_real = jnp.einsum("uckm,mj->uckj", turned_real, cos_in, precision=highest) + jnp.einsum(
        "uckm,mj->uckj", turned_imag, sin_in, precision=highest
    )
    spec_imag = jnp.einsum("uckm,mj->uckj", turned_imag, cos_in, precision=highest) - jnp.einsum(
        "uckm,mj->uckj", turned_real, sin_in, precision=highest
    )
    return spec_real, spec_imag


def inverse_dft(spec_real, spec_imag):
    count, chans, outer, inner = spec_real.shape
    cos_in, sin_in = turn_table(inner, inner, inner, 1.0)
    back_real = jnp.einsum("uckj,jm->uckm", spec_real, cos_in, precision=highest) - jnp.einsum(
        "uckj,jm->uckm", spec_imag, sin_in, precision=highest
    )
    back_imag = jnp.einsum("uckj,jm->uckm", spec_imag, cos_in, precision=highest) + jnp.einsum(
        "uckj,jm->uckm", spec_real, sin_in, precision=highest
    )
    cos_tw, sin_tw = turn_table(outer, inner, outer * inner, 1.0)
    turned_real = back_real * cos_tw - back_imag * sin_tw
    turned_imag = back_imag * cos_tw + back_real * sin_tw
    cos_out, sin_out = turn_table(outer, outer // 2, outer, 1.0)
    grid = jnp.einsum("kn,uckm->ucnm", cos_out, turned_real, precision=highest) - jnp.einsum(
        "kn,uckm->ucnm", sin_out, turned_imag, precision=highest
    )
    return grid.reshape(count, chans, outer * inner // 2) / float(outer * inner)


def per_device(
    inputs, norm_gain, in_weight, short_filter, long_filter, conv_bias, out_weight, out_grad
):
    local_rows = inputs.shape[0]
    model_width = inputs.shape[1]
    slab_width = long_filter.shape[1]
    taps = short_filter.shape[1]
    wide_inputs = inputs.astype(jnp.float32)
    inv_rms = lax.rsqrt(jnp.mean(wide_inputs * wide_inputs, axis=1, keepdims=True) + epsilon)
    normed = (wide_inputs * inv_rms * norm_gain).astype(jnp.bfloat16)
    in_panel, out_panel = (
        lax.all_gather(in_weight.reshape(in_weight.shape[0], -1), "seq", axis=0, tiled=True),
        doubled_gather(out_weight.T, "seq").T,
    )
    in_flat = in_panel.reshape(model_width, 3 * slab_width)
    projected = jnp.dot(normed, in_flat, preferred_element_type=jnp.float32)
    projected = projected.astype(jnp.bfloat16).reshape(local_rows, 3, slab_width)
    upper_rim = passed_along(projected[local_rows - (taps - 1) :], "seq", 1)
    extended = jnp.concatenate([upper_rim, projected], 0).astype(jnp.float32)
    mixed = jnp.zeros((local_rows, 3, slab_width), jnp.float32)
    for offset in range(taps):
        begin = taps - 1 - offset
        mixed = mixed + short_filter[:, offset, :][None] * extended[begin : begin + local_rows]
    query_br = mixed[:, 0]
    key_br = mixed[:, 1]
    value_br = mixed[:, 2]
    product = key_br * value_br
    gate_grad = jnp.dot(out_grad, out_panel.T, preferred_element_type=jnp.float32)
    carried = gate_grad * query_br
    filt_real, filt_imag = forward_dft(to_columns(long_filter.T[None]))
    filt_real, filt_imag = (filt_real[0], filt_imag[0])
    columns = to_columns(jnp.stack([product, carried]).transpose(0, 2, 1))
    all_real, all_imag = forward_dft(columns)
    sig_real, grad_real = (all_real[0], all_real[1])
    sig_imag, grad_imag = (all_imag[0], all_imag[1])
    conv_real = sig_real * filt_real - sig_imag * filt_imag
    conv_imag = sig_real * filt_imag + sig_imag * filt_real
    back_real = grad_real * filt_real + grad_imag * filt_imag
    back_imag = grad_imag * filt_real - grad_real * filt_imag
    pair_real = grad_real * sig_real + grad_imag * sig_imag
    pair_imag = grad_imag * sig_real - grad_real * sig_imag
    outs = inverse_dft(
        jnp.stack([conv_real, back_real, pair_real]), jnp.stack([conv_imag, back_imag, pair_imag])
    )
    returned = to_rows(outs)
    conv_out = returned[0]
    back_conv = returned[1]
    filter_grad = returned[2] * float(local_rows * lax.axis_size("seq")) ** (-0.5)
    biased = conv_out + conv_bias * product
    gated = (query_br * biased).astype(jnp.bfloat16)
    partial_out = jnp.dot(gated, out_panel, preferred_element_type=jnp.float32)
    summed = halved_sum(partial_out.astype(jnp.bfloat16), "ch")
    share = summed.shape[1]
    residual = lax.dynamic_slice_in_dim(wide_inputs, lax.axis_index("ch") * share, share, 1)
    block_out = (residual + summed).astype(jnp.bfloat16)
    source_grad = back_conv + conv_bias * carried
    mixed_grad = jnp.stack([gate_grad * biased, source_grad * value_br, source_grad * key_br], 1)
    lower_rim = passed_along(mixed_grad[: taps - 1], "seq", -1)
    extended_back = jnp.concatenate([mixed_grad, lower_rim], 0)
    proj_grad = jnp.zeros((local_rows, 3, slab_width), jnp.float32)
    for offset in range(taps):
        proj_grad = (
            proj_grad
            + short_filter[:, offset, :][None] * extended_back[offset : offset + local_rows]
        )
    proj_grad = proj_grad.astype(jnp.bfloat16).reshape(local_rows, 3 * slab_width)
    partial_grad = jnp.dot(proj_grad, in_flat.T, preferred_element_type=jnp.float32)
    ch_size = lax.axis_size("ch")
    feature_share = model_width // ch_size
    partial_inner = jnp.sum(partial_grad * (norm_gain * wide_inputs), axis=1, keepdims=True)
    inner_high = partial_inner.astype(jnp.bfloat16)
    inner_low = (partial_inner - inner_high.astype(jnp.float32)).astype(jnp.bfloat16)
    extra = jnp.concatenate(
        [inner_high, inner_low, jnp.zeros((local_rows, 126), jnp.bfloat16)], axis=1
    )
    payload = jnp.concatenate(
        [
            partial_grad.astype(jnp.bfloat16).reshape(local_rows, ch_size, feature_share).transpose(1, 0, 2),
            jnp.broadcast_to(extra[None], (ch_size, local_rows, 128)),
        ],
        axis=2,
    )
    reduced = lax.psum_scatter(payload, "ch", scatter_dimension=0).astype(jnp.float32)
    norm_grad = reduced[:, :feature_share]
    inner_term = (reduced[:, feature_share : feature_share + 1] + reduced[:, feature_share + 1 : feature_share + 2]) / model_width
    feature_begin = lax.axis_index("ch") * feature_share
    gain_share = lax.dynamic_slice_in_dim(norm_gain, feature_begin, feature_share, 0)
    inputs_share = lax.dynamic_slice_in_dim(wide_inputs, feature_begin, feature_share, 1)
    grad_share = lax.dynamic_slice_in_dim(out_grad, feature_begin, feature_share, 1)
    weighted = norm_grad * gain_share
    in_grad_share = (
        grad_share.astype(jnp.float32) + weighted * inv_rms - inputs_share * inv_rms**3 * inner_term
    ).astype(jnp.bfloat16)
    in_grad = doubled_gather(in_grad_share[None], "ch").transpose(1, 0, 2).reshape(local_rows, model_width)
    return (block_out, in_grad, filter_grad)


def solution(mesh):
    return jax.shard_map(
        per_device,
        mesh=mesh,
        in_specs=(
            P("seq", None),
            P(),
            P("seq", None, "ch"),
            P(None, None, "ch"),
            P("seq", "ch"),
            P("ch"),
            P("ch", "seq"),
            P("seq", None),
        ),
        out_specs=(P("seq", "ch"), P("seq", None), P("seq", "ch")),
        check_vma=False,
    )
```

```python
import math

import jax
import jax.numpy as jnp
from jax import lax
from jax.sharding import PartitionSpec as P

epsilon = 1e-05
highest = lax.Precision.HIGHEST


def passed_along(block, axis, distance):
    devices = range(lax.axis_size(axis))
    route = [(i - distance, i) for i in devices if i - distance in devices]
    return lax.ppermute(block, axis, route)


def doubled_gather(block, axis):
    devices = lax.axis_size(axis)
    place = lax.axis_index(axis)
    bits = devices.bit_length() - 1
    assert 1 << bits == devices
    gathered = block
    for bit in reversed(range(bits)):
        route = [(i, i ^ (1 << bit)) for i in range(devices)]
        arrived = lax.ppermute(gathered, axis, route)
        lower = ((place >> bit) & 1) == 0
        gathered = jnp.where(lower, jnp.stack([gathered, arrived]), jnp.stack([arrived, gathered]))
    gathered = gathered.transpose(tuple(reversed(range(bits))) + tuple(range(bits, gathered.ndim)))
    return gathered.reshape((devices * block.shape[0],) + block.shape[1:])


def halved_sum(partial, axis):
    devices = lax.axis_size(axis)
    place = lax.axis_index(axis)
    bits = devices.bit_length() - 1
    assert 1 << bits == devices
    rows, width = partial.shape
    share = width // devices
    held = partial.reshape((rows,) + (2,) * bits + (share,))
    held = held.transpose((0,) + tuple(range(bits, 0, -1)) + (bits + 1,)).astype(jnp.float32)
    for bit in range(bits):
        route = [(i, i ^ (1 << bit)) for i in range(devices)]
        mine = (place >> bit) & 1
        kept = lax.dynamic_index_in_dim(held, mine, 1, keepdims=False)
        given = lax.dynamic_index_in_dim(held, 1 - mine, 1, keepdims=False)
        arrived = lax.ppermute(given.astype(jnp.bfloat16), axis, route)
        held = kept + arrived.astype(jnp.float32)
    return held


def to_columns(signals):
    return lax.all_to_all(signals, "seq", split_axis=1, concat_axis=2, tiled=True)


def to_rows(signals):
    count, chans, seq_total = signals.shape
    devices = lax.axis_size("seq")
    local_rows = seq_total // devices
    pieces = signals.reshape(count, chans, devices, local_rows).transpose(2, 0, 1, 3)
    arrived = lax.all_to_all(pieces, "seq", split_axis=0, concat_axis=0, tiled=True)
    return arrived.transpose(1, 3, 0, 2).reshape(count, local_rows, devices * chans)


def turn_table(rows, cols, period, sign):
    turns = jnp.arange(rows, dtype=jnp.int32)[:, None] * jnp.arange(cols, dtype=jnp.int32)[None, :]
    turns = lax.optimization_barrier(turns)
    phases = sign * 2.0 * math.pi / period * (turns % period).astype(jnp.float32)
    return (jnp.cos(phases), jnp.sin(phases))


def fft_sizes(seq_total):
    total = 2 * seq_total
    inner = 1
    while inner * inner < total:
        inner *= 2
    return total // inner, inner


def forward_dft(signals):
    count, chans, seq_total = signals.shape
    outer, inner = fft_sizes(seq_total)
    grid = signals.reshape(count, chans, outer // 2, inner)
    cos_out, sin_out = turn_table(outer, outer // 2, outer, 1.0)
    first_real = jnp.einsum("kn,ucnm->uckm", cos_out, grid, precision=highest)
    first_imag = -jnp.einsum("kn,ucnm->uckm", sin_out, grid, precision=highest)
    cos_tw, sin_tw = turn_table(outer, inner, outer * inner, 1.0)
    turned_real = first_real * cos_tw + first_imag * sin_tw
    turned_imag = first_imag * cos_tw - first_real * sin_tw
    cos_in, sin_in = turn_table(inner, inner, inner, 1.0)
    spec_real = jnp.einsum("uckm,mj->uckj", turned_real, cos_in, precision=highest) + jnp.einsum(
        "uckm,mj->uckj", turned_imag, sin_in, precision=highest
    )
    spec_imag = jnp.einsum("uckm,mj->uckj", turned_imag, cos_in, precision=highest) - jnp.einsum(
        "uckm,mj->uckj", turned_real, sin_in, precision=highest
    )
    return spec_real, spec_imag


def inverse_dft(spec_real, spec_imag):
    count, chans, outer, inner = spec_real.shape
    cos_in, sin_in = turn_table(inner, inner, inner, 1.0)
    back_real = jnp.einsum("uckj,jm->uckm", spec_real, cos_in, precision=highest) - jnp.einsum(
        "uckj,jm->uckm", spec_imag, sin_in, precision=highest
    )
    back_imag = jnp.einsum("uckj,jm->uckm", spec_imag, cos_in, precision=highest) + jnp.einsum(
        "uckj,jm->uckm", spec_real, sin_in, precision=highest
    )
    cos_tw, sin_tw = turn_table(outer, inner, outer * inner, 1.0)
    turned_real = back_real * cos_tw - back_imag * sin_tw
    turned_imag = back_imag * cos_tw + back_real * sin_tw
    cos_out, sin_out = turn_table(outer, outer // 2, outer, 1.0)
    grid = jnp.einsum("kn,uckm->ucnm", cos_out, turned_real, precision=highest) - jnp.einsum(
        "kn,uckm->ucnm", sin_out, turned_imag, precision=highest
    )
    return grid.reshape(count, chans, outer * inner // 2) / float(outer * inner)


def per_device(
    inputs, norm_gain, in_weight, short_filter, long_filter, conv_bias, out_weight, out_grad
):
    local_rows = inputs.shape[0]
    model_width = inputs.shape[1]
    slab_width = long_filter.shape[1]
    taps = short_filter.shape[1]
    wide_inputs = inputs.astype(jnp.float32)
    inv_rms = lax.rsqrt(jnp.mean(wide_inputs * wide_inputs, axis=1, keepdims=True) + epsilon)
    normed = (wide_inputs * inv_rms * norm_gain).astype(jnp.bfloat16)
    in_panel, out_panel = (
        lax.all_gather(in_weight.reshape(in_weight.shape[0], -1), "seq", axis=0, tiled=True),
        doubled_gather(out_weight.T, "seq").T,
    )
    in_flat = in_panel.reshape(model_width, 3 * slab_width)
    projected = jnp.dot(normed, in_flat, preferred_element_type=jnp.float32)
    projected = projected.astype(jnp.bfloat16).reshape(local_rows, 3, slab_width)
    upper_rim = passed_along(projected[local_rows - (taps - 1) :], "seq", 1)
    extended = jnp.concatenate([upper_rim, projected], 0).astype(jnp.float32)
    mixed = jnp.zeros((local_rows, 3, slab_width), jnp.float32)
    for offset in range(taps):
        begin = taps - 1 - offset
        mixed = mixed + short_filter[:, offset, :][None] * extended[begin : begin + local_rows]
    query_br = mixed[:, 0]
    key_br = mixed[:, 1]
    value_br = mixed[:, 2]
    product = key_br * value_br
    gate_grad = jnp.dot(out_grad, out_panel.T, preferred_element_type=jnp.float32)
    carried = gate_grad * query_br
    filt_real, filt_imag = forward_dft(to_columns(long_filter.T[None]))
    filt_real, filt_imag = (filt_real[0], filt_imag[0])
    columns = to_columns(jnp.stack([product, carried]).transpose(0, 2, 1))
    all_real, all_imag = forward_dft(columns)
    sig_real, grad_real = (all_real[0], all_real[1])
    sig_imag, grad_imag = (all_imag[0], all_imag[1])
    conv_real = sig_real * filt_real - sig_imag * filt_imag
    conv_imag = sig_real * filt_imag + sig_imag * filt_real
    back_real = grad_real * filt_real + grad_imag * filt_imag
    back_imag = grad_imag * filt_real - grad_real * filt_imag
    pair_real = grad_real * sig_real + grad_imag * sig_imag
    pair_imag = grad_imag * sig_real - grad_real * sig_imag
    outs = inverse_dft(
        jnp.stack([conv_real, back_real, pair_real]), jnp.stack([conv_imag, back_imag, pair_imag])
    )
    returned = to_rows(outs)
    conv_out = returned[0]
    back_conv = returned[1]
    filter_grad = returned[2] * float(local_rows * lax.axis_size("seq")) ** (-0.5)
    biased = conv_out + conv_bias * product
    gated = (query_br * biased).astype(jnp.bfloat16)
    partial_out = jnp.dot(gated, out_panel, preferred_element_type=jnp.float32)
    source_grad = back_conv + conv_bias * carried
    mixed_grad = jnp.stack([gate_grad * biased, source_grad * value_br, source_grad * key_br], 1)
    lower_rim = passed_along(mixed_grad[: taps - 1], "seq", -1)
    extended_back = jnp.concatenate([mixed_grad, lower_rim], 0)
    proj_grad = jnp.zeros((local_rows, 3, slab_width), jnp.float32)
    for offset in range(taps):
        proj_grad = (
            proj_grad
            + short_filter[:, offset, :][None] * extended_back[offset : offset + local_rows]
        )
    proj_grad = proj_grad.astype(jnp.bfloat16).reshape(local_rows, 3 * slab_width)
    partial_grad = jnp.dot(proj_grad, in_flat.T, preferred_element_type=jnp.float32)
    ch_size = lax.axis_size("ch")
    feature_share = model_width // ch_size
    partial_inner = jnp.sum(partial_grad * (norm_gain * wide_inputs), axis=1, keepdims=True)
    inner_high = partial_inner.astype(jnp.bfloat16)
    inner_low = (partial_inner - inner_high.astype(jnp.float32)).astype(jnp.bfloat16)
    extra = jnp.concatenate(
        [inner_high, inner_low, jnp.zeros((local_rows, 126), jnp.bfloat16)], axis=1
    )
    payload = jnp.concatenate(
        [
            partial_out.astype(jnp.bfloat16).reshape(local_rows, ch_size, feature_share).transpose(1, 0, 2),
            partial_grad.astype(jnp.bfloat16).reshape(local_rows, ch_size, feature_share).transpose(1, 0, 2),
            jnp.broadcast_to(extra[None], (ch_size, local_rows, 128)),
        ],
        axis=2,
    )
    reduced = lax.psum_scatter(payload, "ch", scatter_dimension=0).astype(jnp.float32)
    summed = reduced[:, :feature_share]
    norm_grad = reduced[:, feature_share : 2 * feature_share]
    inner_at = 2 * feature_share
    inner_term = (reduced[:, inner_at : inner_at + 1] + reduced[:, inner_at + 1 : inner_at + 2]) / model_width
    feature_begin = lax.axis_index("ch") * feature_share
    residual = lax.dynamic_slice_in_dim(wide_inputs, feature_begin, feature_share, 1)
    block_out = (residual + summed).astype(jnp.bfloat16)
    gain_share = lax.dynamic_slice_in_dim(norm_gain, feature_begin, feature_share, 0)
    inputs_share = lax.dynamic_slice_in_dim(wide_inputs, feature_begin, feature_share, 1)
    grad_share = lax.dynamic_slice_in_dim(out_grad, feature_begin, feature_share, 1)
    weighted = norm_grad * gain_share
    in_grad_share = (
        grad_share.astype(jnp.float32) + weighted * inv_rms - inputs_share * inv_rms**3 * inner_term
    ).astype(jnp.bfloat16)
    in_grad = doubled_gather(in_grad_share[None], "ch").transpose(1, 0, 2).reshape(local_rows, model_width)
    return (block_out, in_grad, filter_grad)


def solution(mesh):
    return jax.shard_map(
        per_device,
        mesh=mesh,
        in_specs=(
            P("seq", None),
            P(),
            P("seq", None, "ch"),
            P(None, None, "ch"),
            P("seq", "ch"),
            P("ch"),
            P("ch", "seq"),
            P("seq", None),
        ),
        out_specs=(P("seq", "ch"), P("seq", None), P("seq", "ch")),
        check_vma=False,
    )
```

```python
import math

import jax
import jax.numpy as jnp
from jax import lax
from jax.sharding import PartitionSpec as P

epsilon = 1e-05
highest = lax.Precision.HIGHEST


def passed_along(block, axis, distance):
    devices = range(lax.axis_size(axis))
    route = [(i - distance, i) for i in devices if i - distance in devices]
    return lax.ppermute(block, axis, route)


def doubled_gather(block, axis):
    devices = lax.axis_size(axis)
    place = lax.axis_index(axis)
    bits = devices.bit_length() - 1
    assert 1 << bits == devices
    gathered = block
    for bit in reversed(range(bits)):
        route = [(i, i ^ (1 << bit)) for i in range(devices)]
        arrived = lax.ppermute(gathered, axis, route)
        lower = ((place >> bit) & 1) == 0
        gathered = jnp.where(lower, jnp.stack([gathered, arrived]), jnp.stack([arrived, gathered]))
    gathered = gathered.transpose(tuple(reversed(range(bits))) + tuple(range(bits, gathered.ndim)))
    return gathered.reshape((devices * block.shape[0],) + block.shape[1:])


def halved_sum(partial, axis):
    devices = lax.axis_size(axis)
    place = lax.axis_index(axis)
    bits = devices.bit_length() - 1
    assert 1 << bits == devices
    rows, width = partial.shape
    share = width // devices
    held = partial.reshape((rows,) + (2,) * bits + (share,))
    held = held.transpose((0,) + tuple(range(bits, 0, -1)) + (bits + 1,)).astype(jnp.float32)
    for bit in range(bits):
        route = [(i, i ^ (1 << bit)) for i in range(devices)]
        mine = (place >> bit) & 1
        kept = lax.dynamic_index_in_dim(held, mine, 1, keepdims=False)
        given = lax.dynamic_index_in_dim(held, 1 - mine, 1, keepdims=False)
        arrived = lax.ppermute(given.astype(jnp.bfloat16), axis, route)
        held = kept + arrived.astype(jnp.float32)
    return held


def ring_gather(block, axis):
    devices = lax.axis_size(axis)
    place = lax.axis_index(axis)
    arrived = [block] + [
        lax.ppermute(block, axis, [(i, (i + shift) % devices) for i in range(devices)])
        for shift in range(1, devices)
    ]
    flipped = jnp.stack([arrived[(devices - m) % devices] for m in range(devices)])
    doubled = jnp.concatenate([flipped, flipped], 0)
    return lax.dynamic_slice_in_dim(doubled, (devices - place) % devices, devices, 0)


def to_columns(signals):
    return lax.all_to_all(signals, "seq", split_axis=1, concat_axis=2, tiled=True)


def to_rows(signals):
    count, chans, seq_total = signals.shape
    devices = lax.axis_size("seq")
    local_rows = seq_total // devices
    pieces = signals.reshape(count, chans, devices, local_rows).transpose(2, 0, 1, 3)
    arrived = lax.all_to_all(pieces, "seq", split_axis=0, concat_axis=0, tiled=True)
    return arrived.transpose(1, 3, 0, 2).reshape(count, local_rows, devices * chans)


def turn_table(rows, cols, period, sign):
    turns = jnp.arange(rows, dtype=jnp.int32)[:, None] * jnp.arange(cols, dtype=jnp.int32)[None, :]
    turns = lax.optimization_barrier(turns)
    phases = sign * 2.0 * math.pi / period * (turns % period).astype(jnp.float32)
    return (jnp.cos(phases), jnp.sin(phases))


def fft_sizes(seq_total):
    total = 2 * seq_total
    inner = 1
    while inner * inner < total:
        inner *= 2
    return total // inner, inner


def forward_dft(signals):
    count, chans, seq_total = signals.shape
    outer, inner = fft_sizes(seq_total)
    grid = signals.reshape(count, chans, outer // 2, inner)
    cos_out, sin_out = turn_table(outer, outer // 2, outer, 1.0)
    first_real = jnp.einsum("kn,ucnm->uckm", cos_out, grid, precision=highest)
    first_imag = -jnp.einsum("kn,ucnm->uckm", sin_out, grid, precision=highest)
    cos_tw, sin_tw = turn_table(outer, inner, outer * inner, 1.0)
    turned_real = first_real * cos_tw + first_imag * sin_tw
    turned_imag = first_imag * cos_tw - first_real * sin_tw
    cos_in, sin_in = turn_table(inner, inner, inner, 1.0)
    spec_real = jnp.einsum("uckm,mj->uckj", turned_real, cos_in, precision=highest) + jnp.einsum(
        "uckm,mj->uckj", turned_imag, sin_in, precision=highest
    )
    spec_imag = jnp.einsum("uckm,mj->uckj", turned_imag, cos_in, precision=highest) - jnp.einsum(
        "uckm,mj->uckj", turned_real, sin_in, precision=highest
    )
    return spec_real, spec_imag


def inverse_dft(spec_real, spec_imag):
    count, chans, outer, inner = spec_real.shape
    cos_in, sin_in = turn_table(inner, inner, inner, 1.0)
    back_real = jnp.einsum("uckj,jm->uckm", spec_real, cos_in, precision=highest) - jnp.einsum(
        "uckj,jm->uckm", spec_imag, sin_in, precision=highest
    )
    back_imag = jnp.einsum("uckj,jm->uckm", spec_imag, cos_in, precision=highest) + jnp.einsum(
        "uckj,jm->uckm", spec_real, sin_in, precision=highest
    )
    cos_tw, sin_tw = turn_table(outer, inner, outer * inner, 1.0)
    turned_real = back_real * cos_tw - back_imag * sin_tw
    turned_imag = back_imag * cos_tw + back_real * sin_tw
    cos_out, sin_out = turn_table(outer, outer // 2, outer, 1.0)
    grid = jnp.einsum("kn,uckm->ucnm", cos_out, turned_real, precision=highest) - jnp.einsum(
        "kn,uckm->ucnm", sin_out, turned_imag, precision=highest
    )
    return grid.reshape(count, chans, outer * inner // 2) / float(outer * inner)


def per_device(
    inputs, norm_gain, in_weight, short_filter, long_filter, conv_bias, out_weight, out_grad
):
    local_rows = inputs.shape[0]
    model_width = inputs.shape[1]
    slab_width = long_filter.shape[1]
    taps = short_filter.shape[1]
    wide_inputs = inputs.astype(jnp.float32)
    inv_rms = lax.rsqrt(jnp.mean(wide_inputs * wide_inputs, axis=1, keepdims=True) + epsilon)
    normed = (wide_inputs * inv_rms * norm_gain).astype(jnp.bfloat16)
    in_panel, out_panel = (
        lax.all_gather(in_weight.reshape(in_weight.shape[0], -1), "seq", axis=0, tiled=True),
        doubled_gather(out_weight.T, "seq").T,
    )
    in_flat = in_panel.reshape(model_width, 3 * slab_width)
    projected = jnp.dot(normed, in_flat, preferred_element_type=jnp.float32)
    projected = projected.astype(jnp.bfloat16).reshape(local_rows, 3, slab_width)
    upper_rim = passed_along(projected[local_rows - (taps - 1) :], "seq", 1)
    extended = jnp.concatenate([upper_rim, projected], 0).astype(jnp.float32)
    mixed = jnp.zeros((local_rows, 3, slab_width), jnp.float32)
    for offset in range(taps):
        begin = taps - 1 - offset
        mixed = mixed + short_filter[:, offset, :][None] * extended[begin : begin + local_rows]
    query_br = mixed[:, 0]
    key_br = mixed[:, 1]
    value_br = mixed[:, 2]
    product = key_br * value_br
    gate_grad = jnp.dot(out_grad, out_panel.T, preferred_element_type=jnp.float32)
    carried = gate_grad * query_br
    filt_real, filt_imag = forward_dft(to_columns(long_filter.T[None]))
    filt_real, filt_imag = (filt_real[0], filt_imag[0])
    columns = to_columns(jnp.stack([product, carried]).transpose(0, 2, 1))
    all_real, all_imag = forward_dft(columns)
    sig_real, grad_real = (all_real[0], all_real[1])
    sig_imag, grad_imag = (all_imag[0], all_imag[1])
    conv_real = sig_real * filt_real - sig_imag * filt_imag
    conv_imag = sig_real * filt_imag + sig_imag * filt_real
    back_real = grad_real * filt_real + grad_imag * filt_imag
    back_imag = grad_imag * filt_real - grad_real * filt_imag
    pair_real = grad_real * sig_real + grad_imag * sig_imag
    pair_imag = grad_imag * sig_real - grad_real * sig_imag
    outs = inverse_dft(
        jnp.stack([conv_real, back_real, pair_real]), jnp.stack([conv_imag, back_imag, pair_imag])
    )
    returned = to_rows(outs)
    conv_out = returned[0]
    back_conv = returned[1]
    filter_grad = returned[2] * float(local_rows * lax.axis_size("seq")) ** (-0.5)
    biased = conv_out + conv_bias * product
    gated = (query_br * biased).astype(jnp.bfloat16)
    partial_out = jnp.dot(gated, out_panel, preferred_element_type=jnp.float32)
    source_grad = back_conv + conv_bias * carried
    mixed_grad = jnp.stack([gate_grad * biased, source_grad * value_br, source_grad * key_br], 1)
    lower_rim = passed_along(mixed_grad[: taps - 1], "seq", -1)
    extended_back = jnp.concatenate([mixed_grad, lower_rim], 0)
    proj_grad = jnp.zeros((local_rows, 3, slab_width), jnp.float32)
    for offset in range(taps):
        proj_grad = (
            proj_grad
            + short_filter[:, offset, :][None] * extended_back[offset : offset + local_rows]
        )
    proj_grad = proj_grad.astype(jnp.bfloat16).reshape(local_rows, 3 * slab_width)
    partial_grad = jnp.dot(proj_grad, in_flat.T, preferred_element_type=jnp.float32)
    ch_size = lax.axis_size("ch")
    feature_share = model_width // ch_size
    partial_inner = jnp.sum(partial_grad * (norm_gain * wide_inputs), axis=1, keepdims=True)
    inner_high = partial_inner.astype(jnp.bfloat16)
    inner_low = (partial_inner - inner_high.astype(jnp.float32)).astype(jnp.bfloat16)
    extra = jnp.concatenate(
        [inner_high, inner_low, jnp.zeros((local_rows, 126), jnp.bfloat16)], axis=1
    )
    payload = jnp.concatenate(
        [
            partial_out.astype(jnp.bfloat16).reshape(local_rows, ch_size, feature_share).transpose(1, 0, 2),
            partial_grad.astype(jnp.bfloat16).reshape(local_rows, ch_size, feature_share).transpose(1, 0, 2),
            jnp.broadcast_to(extra[None], (ch_size, local_rows, 128)),
        ],
        axis=2,
    )
    reduced = lax.psum_scatter(payload, "ch", scatter_dimension=0).astype(jnp.float32)
    summed = reduced[:, :feature_share]
    norm_grad = reduced[:, feature_share : 2 * feature_share]
    inner_at = 2 * feature_share
    inner_term = (reduced[:, inner_at : inner_at + 1] + reduced[:, inner_at + 1 : inner_at + 2]) / model_width
    feature_begin = lax.axis_index("ch") * feature_share
    residual = lax.dynamic_slice_in_dim(wide_inputs, feature_begin, feature_share, 1)
    block_out = (residual + summed).astype(jnp.bfloat16)
    gain_share = lax.dynamic_slice_in_dim(norm_gain, feature_begin, feature_share, 0)
    inputs_share = lax.dynamic_slice_in_dim(wide_inputs, feature_begin, feature_share, 1)
    grad_share = lax.dynamic_slice_in_dim(out_grad, feature_begin, feature_share, 1)
    weighted = norm_grad * gain_share
    in_grad_share = (
        grad_share.astype(jnp.float32) + weighted * inv_rms - inputs_share * inv_rms**3 * inner_term
    ).astype(jnp.bfloat16)
    in_grad = ring_gather(in_grad_share, "ch").transpose(1, 0, 2).reshape(local_rows, model_width)
    return (block_out, in_grad, filter_grad)


def solution(mesh):
    return jax.shard_map(
        per_device,
        mesh=mesh,
        in_specs=(
            P("seq", None),
            P(),
            P("seq", None, "ch"),
            P(None, None, "ch"),
            P("seq", "ch"),
            P("ch"),
            P("ch", "seq"),
            P("seq", None),
        ),
        out_specs=(P("seq", "ch"), P("seq", None), P("seq", "ch")),
        check_vma=False,
    )
```

```python
import math

import jax
import jax.numpy as jnp
from jax import lax
from jax.sharding import PartitionSpec as P

epsilon = 1e-05
highest = lax.Precision.HIGHEST


def passed_along(block, axis, distance):
    devices = range(lax.axis_size(axis))
    route = [(i - distance, i) for i in devices if i - distance in devices]
    return lax.ppermute(block, axis, route)


def doubled_gather(block, axis):
    devices = lax.axis_size(axis)
    place = lax.axis_index(axis)
    bits = devices.bit_length() - 1
    assert 1 << bits == devices
    gathered = block
    for bit in reversed(range(bits)):
        route = [(i, i ^ (1 << bit)) for i in range(devices)]
        arrived = lax.ppermute(gathered, axis, route)
        lower = ((place >> bit) & 1) == 0
        gathered = jnp.where(lower, jnp.stack([gathered, arrived]), jnp.stack([arrived, gathered]))
    gathered = gathered.transpose(tuple(reversed(range(bits))) + tuple(range(bits, gathered.ndim)))
    return gathered.reshape((devices * block.shape[0],) + block.shape[1:])


def halved_sum(partial, axis):
    devices = lax.axis_size(axis)
    place = lax.axis_index(axis)
    bits = devices.bit_length() - 1
    assert 1 << bits == devices
    rows, width = partial.shape
    share = width // devices
    held = partial.reshape((rows,) + (2,) * bits + (share,))
    held = held.transpose((0,) + tuple(range(bits, 0, -1)) + (bits + 1,)).astype(jnp.float32)
    for bit in range(bits):
        route = [(i, i ^ (1 << bit)) for i in range(devices)]
        mine = (place >> bit) & 1
        kept = lax.dynamic_index_in_dim(held, mine, 1, keepdims=False)
        given = lax.dynamic_index_in_dim(held, 1 - mine, 1, keepdims=False)
        arrived = lax.ppermute(given.astype(jnp.bfloat16), axis, route)
        held = kept + arrived.astype(jnp.float32)
    return held


def to_columns(signals):
    return lax.all_to_all(signals, "seq", split_axis=1, concat_axis=2, tiled=True)


def to_rows(signals):
    count, chans, seq_total = signals.shape
    devices = lax.axis_size("seq")
    local_rows = seq_total // devices
    pieces = signals.reshape(count, chans, devices, local_rows).transpose(2, 0, 1, 3)
    arrived = lax.all_to_all(pieces, "seq", split_axis=0, concat_axis=0, tiled=True)
    return arrived.transpose(1, 3, 0, 2).reshape(count, local_rows, devices * chans)


def turn_table(rows, cols, period, sign):
    turns = jnp.arange(rows, dtype=jnp.int32)[:, None] * jnp.arange(cols, dtype=jnp.int32)[None, :]
    turns = lax.optimization_barrier(turns)
    phases = sign * 2.0 * math.pi / period * (turns % period).astype(jnp.float32)
    return (jnp.cos(phases), jnp.sin(phases))


def fft_sizes(seq_total):
    total = 2 * seq_total
    inner = 1
    while inner * inner < total:
        inner *= 2
    return total // inner, inner


def forward_dft(signals):
    count, chans, seq_total = signals.shape
    outer, inner = fft_sizes(seq_total)
    grid = signals.reshape(count, chans, outer // 2, inner)
    cos_out, sin_out = turn_table(outer, outer // 2, outer, 1.0)
    first_real = jnp.einsum("kn,ucnm->uckm", cos_out, grid, precision=lax.Precision.HIGH)
    first_imag = -jnp.einsum("kn,ucnm->uckm", sin_out, grid, precision=lax.Precision.HIGH)
    cos_tw, sin_tw = turn_table(outer, inner, outer * inner, 1.0)
    turned_real = first_real * cos_tw + first_imag * sin_tw
    turned_imag = first_imag * cos_tw - first_real * sin_tw
    cos_in, sin_in = turn_table(inner, inner, inner, 1.0)
    spec_real = jnp.einsum("uckm,mj->uckj", turned_real, cos_in, precision=lax.Precision.HIGH) + jnp.einsum(
        "uckm,mj->uckj", turned_imag, sin_in, precision=lax.Precision.HIGH
    )
    spec_imag = jnp.einsum("uckm,mj->uckj", turned_imag, cos_in, precision=lax.Precision.HIGH) - jnp.einsum(
        "uckm,mj->uckj", turned_real, sin_in, precision=lax.Precision.HIGH
    )
    return spec_real, spec_imag


def inverse_dft(spec_real, spec_imag):
    count, chans, outer, inner = spec_real.shape
    cos_in, sin_in = turn_table(inner, inner, inner, 1.0)
    back_real = jnp.einsum("uckj,jm->uckm", spec_real, cos_in, precision=lax.Precision.HIGH) - jnp.einsum(
        "uckj,jm->uckm", spec_imag, sin_in, precision=lax.Precision.HIGH
    )
    back_imag = jnp.einsum("uckj,jm->uckm", spec_imag, cos_in, precision=lax.Precision.HIGH) + jnp.einsum(
        "uckj,jm->uckm", spec_real, sin_in, precision=lax.Precision.HIGH
    )
    cos_tw, sin_tw = turn_table(outer, inner, outer * inner, 1.0)
    turned_real = back_real * cos_tw - back_imag * sin_tw
    turned_imag = back_imag * cos_tw + back_real * sin_tw
    cos_out, sin_out = turn_table(outer, outer // 2, outer, 1.0)
    grid = jnp.einsum("kn,uckm->ucnm", cos_out, turned_real, precision=lax.Precision.HIGH) - jnp.einsum(
        "kn,uckm->ucnm", sin_out, turned_imag, precision=lax.Precision.HIGH
    )
    return grid.reshape(count, chans, outer * inner // 2) / float(outer * inner)


def per_device(
    inputs, norm_gain, in_weight, short_filter, long_filter, conv_bias, out_weight, out_grad
):
    local_rows = inputs.shape[0]
    model_width = inputs.shape[1]
    slab_width = long_filter.shape[1]
    taps = short_filter.shape[1]
    wide_inputs = inputs.astype(jnp.float32)
    inv_rms = lax.rsqrt(jnp.mean(wide_inputs * wide_inputs, axis=1, keepdims=True) + epsilon)
    normed = (wide_inputs * inv_rms * norm_gain).astype(jnp.bfloat16)
    in_panel, out_panel = (
        lax.all_gather(in_weight.reshape(in_weight.shape[0], -1), "seq", axis=0, tiled=True),
        doubled_gather(out_weight.T, "seq").T,
    )
    in_flat = in_panel.reshape(model_width, 3 * slab_width)
    projected = jnp.dot(normed, in_flat, preferred_element_type=jnp.float32)
    projected = projected.astype(jnp.bfloat16).reshape(local_rows, 3, slab_width)
    upper_rim = passed_along(projected[local_rows - (taps - 1) :], "seq", 1)
    extended = jnp.concatenate([upper_rim, projected], 0).astype(jnp.float32)
    mixed = jnp.zeros((local_rows, 3, slab_width), jnp.float32)
    for offset in range(taps):
        begin = taps - 1 - offset
        mixed = mixed + short_filter[:, offset, :][None] * extended[begin : begin + local_rows]
    query_br = mixed[:, 0]
    key_br = mixed[:, 1]
    value_br = mixed[:, 2]
    product = key_br * value_br
    gate_grad = jnp.dot(out_grad, out_panel.T, preferred_element_type=jnp.float32)
    carried = gate_grad * query_br
    filt_real, filt_imag = forward_dft(to_columns(long_filter.T[None]))
    filt_real, filt_imag = (filt_real[0], filt_imag[0])
    columns = to_columns(jnp.stack([product, carried]).transpose(0, 2, 1))
    all_real, all_imag = forward_dft(columns)
    sig_real, grad_real = (all_real[0], all_real[1])
    sig_imag, grad_imag = (all_imag[0], all_imag[1])
    conv_real = sig_real * filt_real - sig_imag * filt_imag
    conv_imag = sig_real * filt_imag + sig_imag * filt_real
    back_real = grad_real * filt_real + grad_imag * filt_imag
    back_imag = grad_imag * filt_real - grad_real * filt_imag
    pair_real = grad_real * sig_real + grad_imag * sig_imag
    pair_imag = grad_imag * sig_real - grad_real * sig_imag
    outs = inverse_dft(
        jnp.stack([conv_real, back_real, pair_real]), jnp.stack([conv_imag, back_imag, pair_imag])
    )
    returned = to_rows(outs)
    conv_out = returned[0]
    back_conv = returned[1]
    filter_grad = returned[2] * float(local_rows * lax.axis_size("seq")) ** (-0.5)
    biased = conv_out + conv_bias * product
    gated = (query_br * biased).astype(jnp.bfloat16)
    partial_out = jnp.dot(gated, out_panel, preferred_element_type=jnp.float32)
    source_grad = back_conv + conv_bias * carried
    mixed_grad = jnp.stack([gate_grad * biased, source_grad * value_br, source_grad * key_br], 1)
    lower_rim = passed_along(mixed_grad[: taps - 1], "seq", -1)
    extended_back = jnp.concatenate([mixed_grad, lower_rim], 0)
    proj_grad = jnp.zeros((local_rows, 3, slab_width), jnp.float32)
    for offset in range(taps):
        proj_grad = (
            proj_grad
            + short_filter[:, offset, :][None] * extended_back[offset : offset + local_rows]
        )
    proj_grad = proj_grad.astype(jnp.bfloat16).reshape(local_rows, 3 * slab_width)
    partial_grad = jnp.dot(proj_grad, in_flat.T, preferred_element_type=jnp.float32)
    ch_size = lax.axis_size("ch")
    feature_share = model_width // ch_size
    partial_inner = jnp.sum(partial_grad * (norm_gain * wide_inputs), axis=1, keepdims=True)
    inner_high = partial_inner.astype(jnp.bfloat16)
    inner_low = (partial_inner - inner_high.astype(jnp.float32)).astype(jnp.bfloat16)
    extra = jnp.concatenate(
        [inner_high, inner_low, jnp.zeros((local_rows, 126), jnp.bfloat16)], axis=1
    )
    payload = jnp.concatenate(
        [
            partial_out.astype(jnp.bfloat16).reshape(local_rows, ch_size, feature_share).transpose(1, 0, 2),
            partial_grad.astype(jnp.bfloat16).reshape(local_rows, ch_size, feature_share).transpose(1, 0, 2),
            jnp.broadcast_to(extra[None], (ch_size, local_rows, 128)),
        ],
        axis=2,
    )
    reduced = lax.psum_scatter(payload, "ch", scatter_dimension=0).astype(jnp.float32)
    summed = reduced[:, :feature_share]
    norm_grad = reduced[:, feature_share : 2 * feature_share]
    inner_at = 2 * feature_share
    inner_term = (reduced[:, inner_at : inner_at + 1] + reduced[:, inner_at + 1 : inner_at + 2]) / model_width
    feature_begin = lax.axis_index("ch") * feature_share
    residual = lax.dynamic_slice_in_dim(wide_inputs, feature_begin, feature_share, 1)
    block_out = (residual + summed).astype(jnp.bfloat16)
    gain_share = lax.dynamic_slice_in_dim(norm_gain, feature_begin, feature_share, 0)
    inputs_share = lax.dynamic_slice_in_dim(wide_inputs, feature_begin, feature_share, 1)
    grad_share = lax.dynamic_slice_in_dim(out_grad, feature_begin, feature_share, 1)
    weighted = norm_grad * gain_share
    in_grad_share = (
        grad_share.astype(jnp.float32) + weighted * inv_rms - inputs_share * inv_rms**3 * inner_term
    ).astype(jnp.bfloat16)
    in_grad = doubled_gather(in_grad_share[None], "ch").transpose(1, 0, 2).reshape(local_rows, model_width)
    return (block_out, in_grad, filter_grad)


def solution(mesh):
    return jax.shard_map(
        per_device,
        mesh=mesh,
        in_specs=(
            P("seq", None),
            P(),
            P("seq", None, "ch"),
            P(None, None, "ch"),
            P("seq", "ch"),
            P("ch"),
            P("ch", "seq"),
            P("seq", None),
        ),
        out_specs=(P("seq", "ch"), P("seq", None), P("seq", "ch")),
        check_vma=False,
    )
```

```python
import math

import jax
import jax.numpy as jnp
from jax import lax
from jax.sharding import PartitionSpec as P

epsilon = 1e-05
highest = lax.Precision.HIGHEST


def passed_along(block, axis, distance):
    devices = range(lax.axis_size(axis))
    route = [(i - distance, i) for i in devices if i - distance in devices]
    return lax.ppermute(block, axis, route)


def doubled_gather(block, axis):
    devices = lax.axis_size(axis)
    place = lax.axis_index(axis)
    bits = devices.bit_length() - 1
    assert 1 << bits == devices
    gathered = block
    for bit in reversed(range(bits)):
        route = [(i, i ^ (1 << bit)) for i in range(devices)]
        arrived = lax.ppermute(gathered, axis, route)
        lower = ((place >> bit) & 1) == 0
        gathered = jnp.where(lower, jnp.stack([gathered, arrived]), jnp.stack([arrived, gathered]))
    gathered = gathered.transpose(tuple(reversed(range(bits))) + tuple(range(bits, gathered.ndim)))
    return gathered.reshape((devices * block.shape[0],) + block.shape[1:])


def halved_sum(partial, axis):
    devices = lax.axis_size(axis)
    place = lax.axis_index(axis)
    bits = devices.bit_length() - 1
    assert 1 << bits == devices
    rows, width = partial.shape
    share = width // devices
    held = partial.reshape((rows,) + (2,) * bits + (share,))
    held = held.transpose((0,) + tuple(range(bits, 0, -1)) + (bits + 1,)).astype(jnp.float32)
    for bit in range(bits):
        route = [(i, i ^ (1 << bit)) for i in range(devices)]
        mine = (place >> bit) & 1
        kept = lax.dynamic_index_in_dim(held, mine, 1, keepdims=False)
        given = lax.dynamic_index_in_dim(held, 1 - mine, 1, keepdims=False)
        arrived = lax.ppermute(given.astype(jnp.bfloat16), axis, route)
        held = kept + arrived.astype(jnp.float32)
    return held


def to_columns(signals):
    return lax.all_to_all(signals, "seq", split_axis=1, concat_axis=2, tiled=True)


def to_rows(signals):
    count, chans, seq_total = signals.shape
    devices = lax.axis_size("seq")
    local_rows = seq_total // devices
    pieces = signals.reshape(count, chans, devices, local_rows).transpose(2, 0, 1, 3)
    arrived = lax.all_to_all(pieces, "seq", split_axis=0, concat_axis=0, tiled=True)
    return arrived.transpose(1, 3, 0, 2).reshape(count, local_rows, devices * chans)


def turn_table(rows, cols, period, sign):
    turns = jnp.arange(rows, dtype=jnp.int32)[:, None] * jnp.arange(cols, dtype=jnp.int32)[None, :]
    turns = lax.optimization_barrier(turns)
    phases = sign * 2.0 * math.pi / period * (turns % period).astype(jnp.float32)
    return (jnp.cos(phases), jnp.sin(phases))


def fft_sizes(seq_total):
    total = 2 * seq_total
    inner = 1
    while inner * inner < total:
        inner *= 2
    return total // inner, inner


def forward_dft(signals):
    count, chans, seq_total = signals.shape
    outer, inner = fft_sizes(seq_total)
    grid = signals.reshape(count, chans, outer // 2, inner)
    cos_out, sin_out = turn_table(outer, outer // 2, outer, 1.0)
    first_real = jnp.einsum("kn,ucnm->uckm", cos_out, grid, precision=lax.Precision.HIGH)
    first_imag = -jnp.einsum("kn,ucnm->uckm", sin_out, grid, precision=lax.Precision.HIGH)
    cos_tw, sin_tw = turn_table(outer, inner, outer * inner, 1.0)
    turned_real = first_real * cos_tw + first_imag * sin_tw
    turned_imag = first_imag * cos_tw - first_real * sin_tw
    cos_in, sin_in = turn_table(inner, inner, inner, 1.0)
    rotation = jnp.concatenate(
        [jnp.concatenate([cos_in, -sin_in], 1), jnp.concatenate([sin_in, cos_in], 1)], 0
    )
    joined = jnp.concatenate([turned_real, turned_imag], -1)
    spec = jnp.einsum("uckm,mj->uckj", joined, rotation, precision=lax.Precision.HIGH)
    return spec[..., :inner], spec[..., inner:]


def inverse_dft(spec_real, spec_imag):
    count, chans, outer, inner = spec_real.shape
    cos_in, sin_in = turn_table(inner, inner, inner, 1.0)
    rotation = jnp.concatenate(
        [jnp.concatenate([cos_in, sin_in], 1), jnp.concatenate([-sin_in, cos_in], 1)], 0
    )
    joined = jnp.concatenate([spec_real, spec_imag], -1)
    back = jnp.einsum("uckj,jm->uckm", joined, rotation, precision=lax.Precision.HIGH)
    back_real, back_imag = back[..., :inner], back[..., inner:]
    cos_tw, sin_tw = turn_table(outer, inner, outer * inner, 1.0)
    turned_real = back_real * cos_tw - back_imag * sin_tw
    turned_imag = back_imag * cos_tw + back_real * sin_tw
    cos_out, sin_out = turn_table(outer, outer // 2, outer, 1.0)
    grid = jnp.einsum("kn,uckm->ucnm", cos_out, turned_real, precision=lax.Precision.HIGH) - jnp.einsum(
        "kn,uckm->ucnm", sin_out, turned_imag, precision=lax.Precision.HIGH
    )
    return grid.reshape(count, chans, outer * inner // 2) / float(outer * inner)


def per_device(
    inputs, norm_gain, in_weight, short_filter, long_filter, conv_bias, out_weight, out_grad
):
    local_rows = inputs.shape[0]
    model_width = inputs.shape[1]
    slab_width = long_filter.shape[1]
    taps = short_filter.shape[1]
    wide_inputs = inputs.astype(jnp.float32)
    inv_rms = lax.rsqrt(jnp.mean(wide_inputs * wide_inputs, axis=1, keepdims=True) + epsilon)
    normed = (wide_inputs * inv_rms * norm_gain).astype(jnp.bfloat16)
    in_panel, out_panel = (
        lax.all_gather(in_weight.reshape(in_weight.shape[0], -1), "seq", axis=0, tiled=True),
        doubled_gather(out_weight.T, "seq").T,
    )
    in_flat = in_panel.reshape(model_width, 3 * slab_width)
    projected = jnp.dot(normed, in_flat, preferred_element_type=jnp.float32)
    projected = projected.astype(jnp.bfloat16).reshape(local_rows, 3, slab_width)
    upper_rim = passed_along(projected[local_rows - (taps - 1) :], "seq", 1)
    extended = jnp.concatenate([upper_rim, projected], 0).astype(jnp.float32)
    mixed = jnp.zeros((local_rows, 3, slab_width), jnp.float32)
    for offset in range(taps):
        begin = taps - 1 - offset
        mixed = mixed + short_filter[:, offset, :][None] * extended[begin : begin + local_rows]
    query_br = mixed[:, 0]
    key_br = mixed[:, 1]
    value_br = mixed[:, 2]
    product = key_br * value_br
    gate_grad = jnp.dot(out_grad, out_panel.T, preferred_element_type=jnp.float32)
    carried = gate_grad * query_br
    filt_real, filt_imag = forward_dft(to_columns(long_filter.T[None]))
    filt_real, filt_imag = (filt_real[0], filt_imag[0])
    columns = to_columns(jnp.stack([product, carried]).transpose(0, 2, 1))
    all_real, all_imag = forward_dft(columns)
    sig_real, grad_real = (all_real[0], all_real[1])
    sig_imag, grad_imag = (all_imag[0], all_imag[1])
    conv_real = sig_real * filt_real - sig_imag * filt_imag
    conv_imag = sig_real * filt_imag + sig_imag * filt_real
    back_real = grad_real * filt_real + grad_imag * filt_imag
    back_imag = grad_imag * filt_real - grad_real * filt_imag
    pair_real = grad_real * sig_real + grad_imag * sig_imag
    pair_imag = grad_imag * sig_real - grad_real * sig_imag
    outs = inverse_dft(
        jnp.stack([conv_real, back_real, pair_real]), jnp.stack([conv_imag, back_imag, pair_imag])
    )
    returned = to_rows(outs)
    conv_out = returned[0]
    back_conv = returned[1]
    filter_grad = returned[2] * float(local_rows * lax.axis_size("seq")) ** (-0.5)
    biased = conv_out + conv_bias * product
    gated = (query_br * biased).astype(jnp.bfloat16)
    partial_out = jnp.dot(gated, out_panel, preferred_element_type=jnp.float32)
    source_grad = back_conv + conv_bias * carried
    mixed_grad = jnp.stack([gate_grad * biased, source_grad * value_br, source_grad * key_br], 1)
    lower_rim = passed_along(mixed_grad[: taps - 1], "seq", -1)
    extended_back = jnp.concatenate([mixed_grad, lower_rim], 0)
    proj_grad = jnp.zeros((local_rows, 3, slab_width), jnp.float32)
    for offset in range(taps):
        proj_grad = (
            proj_grad
            + short_filter[:, offset, :][None] * extended_back[offset : offset + local_rows]
        )
    proj_grad = proj_grad.astype(jnp.bfloat16).reshape(local_rows, 3 * slab_width)
    partial_grad = jnp.dot(proj_grad, in_flat.T, preferred_element_type=jnp.float32)
    ch_size = lax.axis_size("ch")
    feature_share = model_width // ch_size
    partial_inner = jnp.sum(partial_grad * (norm_gain * wide_inputs), axis=1, keepdims=True)
    inner_high = partial_inner.astype(jnp.bfloat16)
    inner_low = (partial_inner - inner_high.astype(jnp.float32)).astype(jnp.bfloat16)
    extra = jnp.concatenate(
        [inner_high, inner_low, jnp.zeros((local_rows, 126), jnp.bfloat16)], axis=1
    )
    payload = jnp.concatenate(
        [
            partial_out.astype(jnp.bfloat16).reshape(local_rows, ch_size, feature_share).transpose(1, 0, 2),
            partial_grad.astype(jnp.bfloat16).reshape(local_rows, ch_size, feature_share).transpose(1, 0, 2),
            jnp.broadcast_to(extra[None], (ch_size, local_rows, 128)),
        ],
        axis=2,
    )
    reduced = lax.psum_scatter(payload, "ch", scatter_dimension=0).astype(jnp.float32)
    summed = reduced[:, :feature_share]
    norm_grad = reduced[:, feature_share : 2 * feature_share]
    inner_at = 2 * feature_share
    inner_term = (reduced[:, inner_at : inner_at + 1] + reduced[:, inner_at + 1 : inner_at + 2]) / model_width
    feature_begin = lax.axis_index("ch") * feature_share
    residual = lax.dynamic_slice_in_dim(wide_inputs, feature_begin, feature_share, 1)
    block_out = (residual + summed).astype(jnp.bfloat16)
    gain_share = lax.dynamic_slice_in_dim(norm_gain, feature_begin, feature_share, 0)
    inputs_share = lax.dynamic_slice_in_dim(wide_inputs, feature_begin, feature_share, 1)
    grad_share = lax.dynamic_slice_in_dim(out_grad, feature_begin, feature_share, 1)
    weighted = norm_grad * gain_share
    in_grad_share = (
        grad_share.astype(jnp.float32) + weighted * inv_rms - inputs_share * inv_rms**3 * inner_term
    ).astype(jnp.bfloat16)
    in_grad = doubled_gather(in_grad_share[None], "ch").transpose(1, 0, 2).reshape(local_rows, model_width)
    return (block_out, in_grad, filter_grad)


def solution(mesh):
    return jax.shard_map(
        per_device,
        mesh=mesh,
        in_specs=(
            P("seq", None),
            P(),
            P("seq", None, "ch"),
            P(None, None, "ch"),
            P("seq", "ch"),
            P("ch"),
            P("ch", "seq"),
            P("seq", None),
        ),
        out_specs=(P("seq", "ch"), P("seq", None), P("seq", "ch")),
        check_vma=False,
    )
```

```python
import math

import jax
import jax.numpy as jnp
from jax import lax
from jax.sharding import PartitionSpec as P

epsilon = 1e-05
highest = lax.Precision.HIGHEST


def passed_along(block, axis, distance):
    devices = range(lax.axis_size(axis))
    route = [(i - distance, i) for i in devices if i - distance in devices]
    return lax.ppermute(block, axis, route)


def doubled_gather(block, axis):
    devices = lax.axis_size(axis)
    place = lax.axis_index(axis)
    bits = devices.bit_length() - 1
    assert 1 << bits == devices
    gathered = block
    for bit in reversed(range(bits)):
        route = [(i, i ^ (1 << bit)) for i in range(devices)]
        arrived = lax.ppermute(gathered, axis, route)
        lower = ((place >> bit) & 1) == 0
        gathered = jnp.where(lower, jnp.stack([gathered, arrived]), jnp.stack([arrived, gathered]))
    gathered = gathered.transpose(tuple(reversed(range(bits))) + tuple(range(bits, gathered.ndim)))
    return gathered.reshape((devices * block.shape[0],) + block.shape[1:])


def halved_sum(partial, axis):
    devices = lax.axis_size(axis)
    place = lax.axis_index(axis)
    bits = devices.bit_length() - 1
    assert 1 << bits == devices
    rows, width = partial.shape
    share = width // devices
    held = partial.reshape((rows,) + (2,) * bits + (share,))
    held = held.transpose((0,) + tuple(range(bits, 0, -1)) + (bits + 1,)).astype(jnp.float32)
    for bit in range(bits):
        route = [(i, i ^ (1 << bit)) for i in range(devices)]
        mine = (place >> bit) & 1
        kept = lax.dynamic_index_in_dim(held, mine, 1, keepdims=False)
        given = lax.dynamic_index_in_dim(held, 1 - mine, 1, keepdims=False)
        arrived = lax.ppermute(given.astype(jnp.bfloat16), axis, route)
        held = kept + arrived.astype(jnp.float32)
    return held


def to_columns(signals):
    return lax.all_to_all(signals, "seq", split_axis=1, concat_axis=2, tiled=True)


def to_rows(signals):
    count, chans, seq_total = signals.shape
    devices = lax.axis_size("seq")
    local_rows = seq_total // devices
    pieces = signals.reshape(count, chans, devices, local_rows).transpose(2, 0, 1, 3)
    arrived = lax.all_to_all(pieces, "seq", split_axis=0, concat_axis=0, tiled=True)
    return arrived.transpose(1, 3, 0, 2).reshape(count, local_rows, devices * chans)


def turn_table(rows, cols, period, sign):
    turns = jnp.arange(rows, dtype=jnp.int32)[:, None] * jnp.arange(cols, dtype=jnp.int32)[None, :]
    turns = lax.optimization_barrier(turns)
    phases = sign * 2.0 * math.pi / period * (turns % period).astype(jnp.float32)
    return (jnp.cos(phases), jnp.sin(phases))


def fft_sizes(seq_total):
    total = 2 * seq_total
    inner = 1
    while inner * inner < total:
        inner *= 2
    return total // inner, inner


def forward_dft(signals):
    count, chans, seq_total = signals.shape
    outer, inner = fft_sizes(seq_total)
    grid = signals.reshape(count, chans, outer // 2, inner)
    cos_out, sin_out = turn_table(outer, outer // 2, outer, 1.0)
    first = jnp.einsum(
        "kn,ucnm->uckm", jnp.concatenate([cos_out, -sin_out], 0), grid, precision=lax.Precision.HIGH
    )
    first_real, first_imag = first[:, :, :outer], first[:, :, outer:]
    cos_tw, sin_tw = turn_table(outer, inner, outer * inner, 1.0)
    turned_real = first_real * cos_tw + first_imag * sin_tw
    turned_imag = first_imag * cos_tw - first_real * sin_tw
    cos_in, sin_in = turn_table(inner, inner, inner, 1.0)
    rotation = jnp.concatenate(
        [jnp.concatenate([cos_in, -sin_in], 1), jnp.concatenate([sin_in, cos_in], 1)], 0
    )
    joined = jnp.concatenate([turned_real, turned_imag], -1)
    spec = jnp.einsum("uckm,mj->uckj", joined, rotation, precision=lax.Precision.HIGH)
    return spec[..., :inner], spec[..., inner:]


def inverse_dft(spec_real, spec_imag):
    count, chans, outer, inner = spec_real.shape
    cos_in, sin_in = turn_table(inner, inner, inner, 1.0)
    rotation = jnp.concatenate(
        [jnp.concatenate([cos_in, sin_in], 1), jnp.concatenate([-sin_in, cos_in], 1)], 0
    )
    joined = jnp.concatenate([spec_real, spec_imag], -1)
    back = jnp.einsum("uckj,jm->uckm", joined, rotation, precision=lax.Precision.HIGH)
    back_real, back_imag = back[..., :inner], back[..., inner:]
    cos_tw, sin_tw = turn_table(outer, inner, outer * inner, 1.0)
    turned_real = back_real * cos_tw - back_imag * sin_tw
    turned_imag = back_imag * cos_tw + back_real * sin_tw
    cos_out, sin_out = turn_table(outer, outer // 2, outer, 1.0)
    grid = jnp.einsum(
        "kn,uckm->ucnm",
        jnp.concatenate([cos_out, -sin_out], 0),
        jnp.concatenate([turned_real, turned_imag], 2),
        precision=lax.Precision.HIGH,
    )
    return grid.reshape(count, chans, outer * inner // 2) / float(outer * inner)


def per_device(
    inputs, norm_gain, in_weight, short_filter, long_filter, conv_bias, out_weight, out_grad
):
    local_rows = inputs.shape[0]
    model_width = inputs.shape[1]
    slab_width = long_filter.shape[1]
    taps = short_filter.shape[1]
    wide_inputs = inputs.astype(jnp.float32)
    inv_rms = lax.rsqrt(jnp.mean(wide_inputs * wide_inputs, axis=1, keepdims=True) + epsilon)
    normed = (wide_inputs * inv_rms * norm_gain).astype(jnp.bfloat16)
    in_panel, out_panel = (
        lax.all_gather(in_weight.reshape(in_weight.shape[0], -1), "seq", axis=0, tiled=True),
        doubled_gather(out_weight.T, "seq").T,
    )
    in_flat = in_panel.reshape(model_width, 3 * slab_width)
    projected = jnp.dot(normed, in_flat, preferred_element_type=jnp.float32)
    projected = projected.astype(jnp.bfloat16).reshape(local_rows, 3, slab_width)
    upper_rim = passed_along(projected[local_rows - (taps - 1) :], "seq", 1)
    extended = jnp.concatenate([upper_rim, projected], 0).astype(jnp.float32)
    mixed = jnp.zeros((local_rows, 3, slab_width), jnp.float32)
    for offset in range(taps):
        begin = taps - 1 - offset
        mixed = mixed + short_filter[:, offset, :][None] * extended[begin : begin + local_rows]
    query_br = mixed[:, 0]
    key_br = mixed[:, 1]
    value_br = mixed[:, 2]
    product = key_br * value_br
    gate_grad = jnp.dot(out_grad, out_panel.T, preferred_element_type=jnp.float32)
    carried = gate_grad * query_br
    filt_real, filt_imag = forward_dft(to_columns(long_filter.T[None]))
    filt_real, filt_imag = (filt_real[0], filt_imag[0])
    columns = to_columns(jnp.stack([product, carried]).transpose(0, 2, 1))
    all_real, all_imag = forward_dft(columns)
    sig_real, grad_real = (all_real[0], all_real[1])
    sig_imag, grad_imag = (all_imag[0], all_imag[1])
    conv_real = sig_real * filt_real - sig_imag * filt_imag
    conv_imag = sig_real * filt_imag + sig_imag * filt_real
    back_real = grad_real * filt_real + grad_imag * filt_imag
    back_imag = grad_imag * filt_real - grad_real * filt_imag
    pair_real = grad_real * sig_real + grad_imag * sig_imag
    pair_imag = grad_imag * sig_real - grad_real * sig_imag
    outs = inverse_dft(
        jnp.stack([conv_real, back_real, pair_real]), jnp.stack([conv_imag, back_imag, pair_imag])
    )
    returned = to_rows(outs)
    conv_out = returned[0]
    back_conv = returned[1]
    filter_grad = returned[2] * float(local_rows * lax.axis_size("seq")) ** (-0.5)
    biased = conv_out + conv_bias * product
    gated = (query_br * biased).astype(jnp.bfloat16)
    partial_out = jnp.dot(gated, out_panel, preferred_element_type=jnp.float32)
    source_grad = back_conv + conv_bias * carried
    mixed_grad = jnp.stack([gate_grad * biased, source_grad * value_br, source_grad * key_br], 1)
    lower_rim = passed_along(mixed_grad[: taps - 1], "seq", -1)
    extended_back = jnp.concatenate([mixed_grad, lower_rim], 0)
    proj_grad = jnp.zeros((local_rows, 3, slab_width), jnp.float32)
    for offset in range(taps):
        proj_grad = (
            proj_grad
            + short_filter[:, offset, :][None] * extended_back[offset : offset + local_rows]
        )
    proj_grad = proj_grad.astype(jnp.bfloat16).reshape(local_rows, 3 * slab_width)
    partial_grad = jnp.dot(proj_grad, in_flat.T, preferred_element_type=jnp.float32)
    ch_size = lax.axis_size("ch")
    feature_share = model_width // ch_size
    partial_inner = jnp.sum(partial_grad * (norm_gain * wide_inputs), axis=1, keepdims=True)
    inner_high = partial_inner.astype(jnp.bfloat16)
    inner_low = (partial_inner - inner_high.astype(jnp.float32)).astype(jnp.bfloat16)
    extra = jnp.concatenate(
        [inner_high, inner_low, jnp.zeros((local_rows, 126), jnp.bfloat16)], axis=1
    )
    payload = jnp.concatenate(
        [
            partial_out.astype(jnp.bfloat16).reshape(local_rows, ch_size, feature_share).transpose(1, 0, 2),
            partial_grad.astype(jnp.bfloat16).reshape(local_rows, ch_size, feature_share).transpose(1, 0, 2),
            jnp.broadcast_to(extra[None], (ch_size, local_rows, 128)),
        ],
        axis=2,
    )
    reduced = lax.psum_scatter(payload, "ch", scatter_dimension=0).astype(jnp.float32)
    summed = reduced[:, :feature_share]
    norm_grad = reduced[:, feature_share : 2 * feature_share]
    inner_at = 2 * feature_share
    inner_term = (reduced[:, inner_at : inner_at + 1] + reduced[:, inner_at + 1 : inner_at + 2]) / model_width
    feature_begin = lax.axis_index("ch") * feature_share
    residual = lax.dynamic_slice_in_dim(wide_inputs, feature_begin, feature_share, 1)
    block_out = (residual + summed).astype(jnp.bfloat16)
    gain_share = lax.dynamic_slice_in_dim(norm_gain, feature_begin, feature_share, 0)
    inputs_share = lax.dynamic_slice_in_dim(wide_inputs, feature_begin, feature_share, 1)
    grad_share = lax.dynamic_slice_in_dim(out_grad, feature_begin, feature_share, 1)
    weighted = norm_grad * gain_share
    in_grad_share = (
        grad_share.astype(jnp.float32) + weighted * inv_rms - inputs_share * inv_rms**3 * inner_term
    ).astype(jnp.bfloat16)
    in_grad = doubled_gather(in_grad_share[None], "ch").transpose(1, 0, 2).reshape(local_rows, model_width)
    return (block_out, in_grad, filter_grad)


def solution(mesh):
    return jax.shard_map(
        per_device,
        mesh=mesh,
        in_specs=(
            P("seq", None),
            P(),
            P("seq", None, "ch"),
            P(None, None, "ch"),
            P("seq", "ch"),
            P("ch"),
            P("ch", "seq"),
            P("seq", None),
        ),
        out_specs=(P("seq", "ch"), P("seq", None), P("seq", "ch")),
        check_vma=False,
    )
```
